256 devices in a mesh: row: 64 (over x, z_hi, y), col: 4 (over z_lo, core).
Axes of the slice: x: 4, y: 4, z: 8 (z_hi: 4, z_lo: 2; z = z_hi * 2 + z_lo), core: 2. Of those that a mesh axis runs over, the one named last changes fastest.
Arguments:
- img_hidden: bfloat16 [8, 1536, 2432], P(None, 'row', 'col'), may hold values from -6 to 6
- txt_hidden: bfloat16 [8, 128, 2432], P(None, 'row', 'col'), may hold values from -6 to 6
- latent: float32 [8, 1536, 64], P(None, 'row'), may hold values from -6 to 6
- img_mod: float32 [8, 5, 2432], replicated, may hold values from -4 to 4
- txt_mod: float32 [8, 2, 2432], replicated, may hold values from -4 to 4
- qkv_weight: bfloat16 [3, 2432, 2048], P(None, None, 'col'), may hold values from -0.125 to 0.125
- txt_kv_weight: bfloat16 [2, 2432, 2048], P(None, None, 'col'), may hold values from -0.125 to 0.125
- out_weight: bfloat16 [2048, 2432], P('col', 'row'), may hold values from -0.125 to 0.125
- final_weight: bfloat16 [2432, 64], P('col'), may hold values from -0.125 to 0.125
- qk_gains: float32 [3, 64], replicated, may hold values from 1.5 to 9
- txt_len: int32 [8], replicated, may hold values from 1 to 128, as said below
- step_idx: int32 [8], replicated, may hold values from 1 to 28
Outputs:
- advanced: float32 [8, 1536, 64], P(None, 'row')
- denoised: float32 [8, 1536, 64], P(None, 'row')
The draws below stay inside these ranges and needn't reach their ends.
Inputs may be any that keep to these rules, and one draw needn't show every extreme that they name: `txt_len`: some request has all 128 text tokens live.
All inputs are finite; a program needn't handle non-finite values.
Results may differ from the reference program's by a relative error of at most 0.0044.
The reference program's roundings to bfloat16 on the way count: a program that leaves them out, or rounds other values in their place, can miss the bound.
Values may be sent and summed in bfloat16 or wider, within the bound.
No kernel may reach another device: no remote copies, remote signals or barrier semaphores. Data moves between devices by JAX's collectives and lax.ppermute only.
A program may use at most 128 MiB of HBM per device.

```python
import jax
import jax.numpy as jnp
from jax import lax

D = 2432
HD = 64
HEADS = 32
PC = 64
REQ = 8
TXT = 128
STEPS = 28
IMG = 1536
AD = 2048


def draw_qk_gains(key, part):
    return jax.random.uniform(key, (3, HD), jnp.float32, 1.5, 2.5)


def draw_txt_len(key, part):
    key_lengths = jax.random.fold_in(key, 11)
    key_full = jax.random.fold_in(key, 23)
    lengths = jax.random.randint(key_lengths, (REQ,), 1, TXT + 1)
    full_index = jax.random.randint(key_full, (), 0, REQ)
    return jnp.where(jnp.arange(REQ) == full_index, TXT, lengths).astype(jnp.int32)


def with_ends(drawn, stream_key, low, high):
    longest = drawn.shape.index(max(drawn.shape))
    spots = []
    for shift in (0, 1):
        where = [jax.random.randint(jax.random.fold_in(stream_key, axis), (), 0, length) for axis, length in enumerate(drawn.shape)]
        where[longest] = (where[longest] + shift) % drawn.shape[longest]
        spots.append(tuple(where))
    return drawn.at[spots[0]].set(low).at[spots[1]].set(high)


def level_of(own_key, dims, cuts, smallest, top_value):
    gain, own = 1.0, jax.random.fold_in(own_key, 6)
    for axis_at, shards_of in cuts:
        steps = jnp.exp(jax.random.uniform(jax.random.fold_in(own, axis_at), (shards_of,), jnp.float32, smallest / len(cuts), top_value / len(cuts)))
        gain = gain * jnp.repeat(steps, dims[axis_at] // shards_of).reshape([-1 if axis == axis_at else 1 for axis in range(len(dims))])
    return gain


def bell_draw(rng, extent, spread, limit, pieces=(), held_as=jnp.bfloat16):
    factor_of = level_of(rng, extent, pieces, -0.22, 0.18) if pieces else 1.0
    values = jax.random.normal(rng, extent, jnp.float32) * spread * factor_of
    return jnp.minimum(jnp.maximum(values, -limit), limit).astype(held_as)


def setup_inputs(seed: int = 0) -> dict:
    keys = jax.random.split(jax.random.key(seed), 13)
    return {
        "img_hidden": bell_draw(keys[0], (REQ, IMG, D), 1.0, 6.0, ((1, 64), (2, 4))),
        "txt_hidden": bell_draw(keys[1], (REQ, TXT, D), 1.0, 6.0, ((1, 64), (2, 4))),
        "latent": bell_draw(keys[2], (REQ, IMG, PC), 1.0, 6.0, ((1, 64),), jnp.float32),
        "img_mod": bell_draw(keys[3], (REQ, 5, D), 0.6, 4.0, (), jnp.float32),
        "txt_mod": bell_draw(keys[4], (REQ, 2, D), 0.6, 4.0, (), jnp.float32),
        "qkv_weight": bell_draw(keys[5], (3, D, AD), D ** -0.5, 0.125, ((2, 4),)),
        "txt_kv_weight": bell_draw(keys[6], (2, D, AD), D ** -0.5, 0.125, ((2, 4),)),
        "out_weight": bell_draw(keys[7], (AD, D), AD ** -0.5, 0.125, ((0, 4), (1, 64))),
        "final_weight": bell_draw(keys[8], (D, PC), D ** -0.5, 0.125, ((0, 4),)),
        "qk_gains": draw_qk_gains(jax.random.fold_in(keys[12], 71), 0),
        "txt_len": draw_txt_len(jax.random.fold_in(keys[12], 71), 0),
        "step_idx": with_ends(jax.random.randint(keys[11], (REQ,), 1, STEPS + 1), jax.random.fold_in(keys[11], 1), 1, STEPS).astype(jnp.int32),
    }


def layer_norm(values):
    average = lax.optimization_barrier(jnp.mean(values, -1, keepdims=True))
    centred = values - average
    variance = lax.optimization_barrier(jnp.mean(centred * centred, -1, keepdims=True))
    return centred * lax.rsqrt(variance + 1e-06)

def rms_heads(values, scaling):
    reshaped = values.reshape(values.shape[:-1] + (values.shape[-1] // HD, HD))
    inverse = lax.rsqrt(lax.optimization_barrier(jnp.mean(reshaped * reshaped, -1, keepdims=True)) + 1e-06)
    return (reshaped * inverse * scaling).astype(jnp.bfloat16)

def sigma_at(indices):
    fraction = indices.astype(jnp.float32) / STEPS
    return 3.0 * fraction / (1.0 + 2.0 * fraction)

def one_request(bundle):
    query_rows, key_rows, value_rows, allowed = bundle
    scores = jnp.einsum('qhd,khd->qhk', query_rows.astype(jnp.float32), key_rows.astype(jnp.float32)) * HD ** (-0.5)
    scores = jnp.where(allowed[None, None, :], scores, -1e+30)
    top_score = lax.optimization_barrier(jnp.max(scores, -1, keepdims=True))
    exp_scores = jnp.where(allowed[None, None, :], jnp.exp(scores - top_score), 0.0)
    row_total = lax.optimization_barrier(jnp.sum(exp_scores, -1, keepdims=True))
    rounded = lax.optimization_barrier(exp_scores.astype(jnp.bfloat16)).astype(jnp.float32)
    weighted = jnp.einsum('qhk,khd->qhd', rounded, value_rows.astype(jnp.float32))
    return (weighted / row_total).astype(jnp.bfloat16)

def reference(img_hidden, txt_hidden, latent, img_mod, txt_mod, qkv_weight, txt_kv_weight, out_weight, final_weight, qk_gains, txt_len, step_idx):
    img_wide = img_hidden.astype(jnp.float32)
    normed = (layer_norm(img_wide) * (1.0 + img_mod[:, 1:2, :]) + img_mod[:, 0:1, :]).astype(jnp.bfloat16)
    flat_rows = normed.reshape(REQ * IMG, D)
    queries = rms_heads(jnp.dot(flat_rows, qkv_weight[0], preferred_element_type=jnp.float32), qk_gains[0]).reshape(REQ, IMG, HEADS, HD)
    img_keys = rms_heads(jnp.dot(flat_rows, qkv_weight[1], preferred_element_type=jnp.float32), qk_gains[1]).reshape(REQ, IMG, HEADS, HD)
    img_values = jnp.dot(flat_rows, qkv_weight[2], preferred_element_type=jnp.float32).astype(jnp.bfloat16).reshape(REQ, IMG, HEADS, HD)
    text_normed = (layer_norm(txt_hidden.astype(jnp.float32)) * (1.0 + txt_mod[:, 1:2, :]) + txt_mod[:, 0:1, :]).astype(jnp.bfloat16)
    text_flat = text_normed.reshape(REQ * TXT, D)
    text_keys = rms_heads(jnp.dot(text_flat, txt_kv_weight[0], preferred_element_type=jnp.float32), qk_gains[2]).reshape(REQ, TXT, HEADS, HD)
    text_values = jnp.dot(text_flat, txt_kv_weight[1], preferred_element_type=jnp.float32).astype(jnp.bfloat16).reshape(REQ, TXT, HEADS, HD)
    key_rows = jnp.concatenate([img_keys, text_keys], 1)
    value_rows = jnp.concatenate([img_values, text_values], 1)
    image_live = jnp.zeros((REQ, IMG), jnp.int32) == 0
    text_live = jnp.arange(TXT, dtype=jnp.int32)[None, :] < txt_len[:, None]
    allowed = jnp.concatenate([image_live, text_live], 1)
    attended = lax.map(one_request, (queries, key_rows, value_rows, allowed))
    branch = jnp.dot(attended.reshape(REQ * IMG, AD), out_weight, preferred_element_type=jnp.float32).reshape(REQ, IMG, D)
    mixed = img_wide + img_mod[:, 2:3, :] * branch
    modulated = (layer_norm(mixed) * (1.0 + img_mod[:, 4:5, :]) + img_mod[:, 3:4, :]).astype(jnp.bfloat16)
    velocity = jnp.dot(modulated.reshape(REQ * IMG, D), final_weight, preferred_element_type=jnp.float32).reshape(REQ, IMG, PC)
    sigma_now = sigma_at(step_idx)[:, None, None]
    sigma_next = sigma_at(step_idx - 1)[:, None, None]
    advanced = latent + (sigma_next - sigma_now) * velocity
    denoised = latent - sigma_now * velocity
    return (advanced, denoised)
```

```python
import jax
import jax.numpy as jnp
from jax import lax
from jax.sharding import Mesh
from jax.sharding import PartitionSpec as P

D = 2432
HD = 64
STEPS = 28
REQ = 8

ROW = ("rq", "rm")

eps_norm = 1e-06
neg_fill = -1e30


def layer_norm(values):
    average = jnp.mean(values, -1, keepdims=True)
    centred = values - average
    variance = jnp.mean(centred * centred, -1, keepdims=True)
    return centred * lax.rsqrt(variance + eps_norm)


def rms_heads(values, scaling):
    reshaped = values.reshape(values.shape[:-1] + (values.shape[-1] // HD, HD))
    inverse = lax.rsqrt(jnp.mean(reshaped * reshaped, -1, keepdims=True) + eps_norm)
    return (reshaped * inverse * scaling).astype(jnp.bfloat16)


def sigma_at(indices):
    fraction = indices.astype(jnp.float32) / STEPS
    return 3.0 * fraction / (1.0 + 2.0 * fraction)


def gather_features(local):
    stacked = lax.all_gather(local, "col", axis=0, tiled=False)
    slabs = stacked.shape[0]
    moved = jnp.moveaxis(stacked, 0, -2)
    return moved.reshape(local.shape[:-1] + (slabs * local.shape[-1],))


def attend_one(queries, keys, values, allowed):
    scores = jnp.einsum(
        "qhd,khd->hqk", queries, keys, preferred_element_type=jnp.float32
    ) * HD ** (-0.5)
    scores = jnp.where(allowed[None, None, :], scores, neg_fill)
    top_score = jnp.max(scores, -1, keepdims=True)
    exp_scores = jnp.where(allowed[None, None, :], jnp.exp(scores - top_score), 0.0)
    row_total = jnp.sum(exp_scores, -1)
    weighted = jnp.einsum(
        "hqk,khd->qhd",
        exp_scores.astype(jnp.bfloat16),
        values,
        preferred_element_type=jnp.float32,
    )
    return (weighted / jnp.transpose(row_total)[..., None]).astype(jnp.bfloat16)


def per_device(
    img_hidden,
    txt_hidden,
    latent,
    img_mod,
    txt_mod,
    qkv_weight,
    txt_kv_weight,
    out_weight,
    final_weight,
    qk_gains,
    txt_len,
    step_idx,
):
    requests = img_hidden.shape[0]
    patches = img_hidden.shape[1]
    text_rows = txt_hidden.shape[1]
    cols_local = qkv_weight.shape[2]
    heads_local = cols_local // HD
    block_len = patches + text_rows
    groups = lax.axis_size("rq")
    members = lax.axis_size("rm")

    weight_t = lax.all_gather(jnp.transpose(out_weight), ROW, axis=0, tiled=True)

    img_full = gather_features(img_hidden)
    txt_full = gather_features(txt_hidden)
    img_wide = img_full.astype(jnp.float32)
    normed = (layer_norm(img_wide) * (1.0 + img_mod[:, 1:2, :]) + img_mod[:, 0:1, :]).astype(
        jnp.bfloat16
    )
    flat_rows = normed.reshape(requests * patches, D)
    projected = jnp.einsum("td,cde->cte", flat_rows, qkv_weight, preferred_element_type=jnp.float32)
    queries = rms_heads(projected[0], qk_gains[0]).reshape(requests, patches, cols_local)
    img_keys = rms_heads(projected[1], qk_gains[1]).reshape(requests, patches, cols_local)
    img_values = projected[2].astype(jnp.bfloat16).reshape(requests, patches, cols_local)
    text_normed = (
        layer_norm(txt_full.astype(jnp.float32)) * (1.0 + txt_mod[:, 1:2, :]) + txt_mod[:, 0:1, :]
    ).astype(jnp.bfloat16)
    text_proj = jnp.einsum(
        "rtd,cde->crte", text_normed, txt_kv_weight, preferred_element_type=jnp.float32
    )
    text_keys = rms_heads(text_proj[0], qk_gains[2]).reshape(requests, text_rows, cols_local)
    text_values = text_proj[1].astype(jnp.bfloat16)
    key_rows = jnp.concatenate([img_keys, text_keys], 1)
    value_rows = jnp.concatenate([img_values, text_values], 1)
    kv_rows = jnp.stack([key_rows, value_rows], 1)

    group_queries = lax.all_to_all(queries, "rq", 0, 0, tiled=True)
    group_kv = lax.all_to_all(kv_rows, "rq", 0, 0, tiled=True)
    all_kv = lax.all_gather(group_kv, "rm", axis=0, tiled=False)

    key_count = members * groups * block_len
    keys = all_kv[:, :, 0].reshape(key_count, heads_local, HD)
    values = all_kv[:, :, 1].reshape(key_count, heads_local, HD)

    request = lax.axis_index("rq")
    positions = jnp.arange(key_count, dtype=jnp.int32)
    within = positions % block_len
    source_block = positions // block_len
    member_of = source_block // groups
    group_of = source_block % groups
    source_row = group_of * members + member_of
    text_pos = source_row * text_rows + within - patches
    live_text = text_pos < lax.dynamic_index_in_dim(txt_len, request, keepdims=False)
    allowed = (within < patches) | live_text

    attended = attend_one(
        group_queries.reshape(groups * patches, heads_local, HD), keys, values, allowed
    ).reshape(groups, patches, cols_local)
    attended = lax.all_to_all(attended, "rq", 0, 0, tiled=True).reshape(
        requests * patches, cols_local
    )

    partial_value = lax.dot_general(
        attended,
        weight_t,
        (((1,), (1,)), ((), ())),
        preferred_element_type=jnp.float32,
    )
    slab_width = img_hidden.shape[2]
    col_index = lax.axis_index("col")
    shared_sum = lax.psum_scatter(partial_value, "col", scatter_dimension=1, tiled=True)
    col_mods = lax.dynamic_slice_in_dim(img_mod, col_index * slab_width, slab_width, 2)
    mixed = img_hidden.astype(jnp.float32) + col_mods[:, 2:3, :] * shared_sum.reshape(
        requests, patches, slab_width
    )
    row_sums, squares = lax.psum((jnp.sum(mixed, -1), jnp.sum(mixed * mixed, -1)), "col")
    row_mean = row_sums / D
    spread = squares / D - row_mean * row_mean
    scaled = (mixed - row_mean[..., None]) * lax.rsqrt(spread[..., None] + eps_norm)
    modulated = (scaled * (1.0 + col_mods[:, 4:5, :]) + col_mods[:, 3:4, :]).astype(jnp.bfloat16)
    velocity = lax.psum(
        jnp.dot(
            modulated.reshape(requests * patches, slab_width),
            final_weight,
            preferred_element_type=jnp.float32,
        ),
        "col",
    )
    velocity = velocity.reshape(requests, patches, latent.shape[2])
    sigma_now = sigma_at(step_idx)[:, None, None]
    sigma_next = sigma_at(step_idx - 1)[:, None, None]
    advanced = latent + (sigma_next - sigma_now) * velocity
    denoised = latent - sigma_now * velocity
    return (advanced, denoised)


def solution(mesh):
    rows = mesh.shape["row"]
    cols = mesh.shape["col"]
    split = Mesh(mesh.devices.reshape(REQ, rows // REQ, cols), ("rq", "rm", "col"))
    in_specs = (
        P(None, ROW, "col"),
        P(None, ROW, "col"),
        P(None, ROW, None),
        P(),
        P(),
        P(None, None, "col"),
        P(None, None, "col"),
        P("col", ROW),
        P("col", None),
        P(),
        P(),
        P(),
    )
    out_specs = (P(None, ROW, None), P(None, ROW, None))
    return jax.shard_map(
        per_device, mesh=split, in_specs=in_specs, out_specs=out_specs, check_vma=False
    )
```

```python
import jax
import jax.numpy as jnp
from jax import lax
from jax.sharding import Mesh
from jax.sharding import PartitionSpec as P

D = 2432
HD = 64
STEPS = 28
REQ = 8

ROW = ("rq", "rm")

eps_norm = 1e-06
neg_fill = -1e30


def layer_norm(values):
    average = jnp.mean(values, -1, keepdims=True)
    centred = values - average
    variance = jnp.mean(centred * centred, -1, keepdims=True)
    return centred * lax.rsqrt(variance + eps_norm)


def rms_heads(values, scaling):
    reshaped = values.reshape(values.shape[:-1] + (values.shape[-1] // HD, HD))
    inverse = lax.rsqrt(jnp.mean(reshaped * reshaped, -1, keepdims=True) + eps_norm)
    return (reshaped * inverse * scaling).astype(jnp.bfloat16)


def sigma_at(indices):
    fraction = indices.astype(jnp.float32) / STEPS
    return 3.0 * fraction / (1.0 + 2.0 * fraction)


def gather_features(local):
    stacked = lax.all_gather(local, "col", axis=0, tiled=False)
    slabs = stacked.shape[0]
    moved = jnp.moveaxis(stacked, 0, -2)
    return moved.reshape(local.shape[:-1] + (slabs * local.shape[-1],))


def attend_one(queries, keys, values, allowed):
    scores = jnp.dot(queries, keys.T, preferred_element_type=jnp.float32) * HD ** (-0.5)
    scores = jnp.where(allowed[None, :], scores, neg_fill)
    top_score = jnp.max(scores, -1, keepdims=True)
    exp_scores = jnp.where(allowed[None, :], jnp.exp(scores - top_score), 0.0)
    row_total = jnp.sum(exp_scores, -1, keepdims=True)
    weighted = jnp.dot(exp_scores.astype(jnp.bfloat16), values, preferred_element_type=jnp.float32)
    return (weighted / row_total).astype(jnp.bfloat16)


def per_device(
    img_hidden,
    txt_hidden,
    latent,
    img_mod,
    txt_mod,
    qkv_weight,
    txt_kv_weight,
    out_weight,
    final_weight,
    qk_gains,
    txt_len,
    step_idx,
):
    requests = img_hidden.shape[0]
    patches = img_hidden.shape[1]
    text_rows = txt_hidden.shape[1]
    cols_local = qkv_weight.shape[2]
    heads_local = cols_local // HD
    block_len = patches + text_rows

    weight_t = lax.all_gather(jnp.transpose(out_weight), ROW, axis=0, tiled=True)

    img_full = gather_features(img_hidden)
    txt_full = gather_features(txt_hidden)
    img_wide = img_full.astype(jnp.float32)
    normed = (layer_norm(img_wide) * (1.0 + img_mod[:, 1:2, :]) + img_mod[:, 0:1, :]).astype(
        jnp.bfloat16
    )
    flat_rows = normed.reshape(requests * patches, D)
    projected = jnp.einsum("td,cde->cte", flat_rows, qkv_weight, preferred_element_type=jnp.float32)
    queries = rms_heads(projected[0], qk_gains[0]).reshape(requests, patches, cols_local)
    img_keys = rms_heads(projected[1], qk_gains[1]).reshape(requests, patches, cols_local)
    img_values = projected[2].astype(jnp.bfloat16).reshape(requests, patches, cols_local)
    text_normed = (
        layer_norm(txt_full.astype(jnp.float32)) * (1.0 + txt_mod[:, 1:2, :]) + txt_mod[:, 0:1, :]
    ).astype(jnp.bfloat16)
    text_proj = jnp.einsum(
        "rtd,cde->crte", text_normed, txt_kv_weight, preferred_element_type=jnp.float32
    )
    text_keys = rms_heads(text_proj[0], qk_gains[2]).reshape(requests, text_rows, cols_local)
    text_values = text_proj[1].astype(jnp.bfloat16)
    key_rows = jnp.concatenate([img_keys, text_keys], 1)
    value_rows = jnp.concatenate([img_values, text_values], 1)

    def by_head(values, length):
        split = values.reshape(requests, length, heads_local, HD)
        return jnp.transpose(split, (0, 2, 1, 3)).reshape(requests * heads_local, length, HD)

    bundle = jnp.concatenate(
        [by_head(queries, patches), by_head(key_rows, block_len), by_head(value_rows, block_len)], 1
    )
    bundle = lax.all_to_all(bundle, ROW, 0, 0, tiled=True)
    sources = bundle.shape[0]
    head_queries = bundle[:, :patches].reshape(sources * patches, HD)
    keys = bundle[:, patches : patches + block_len].reshape(sources * block_len, HD)
    values = bundle[:, patches + block_len :].reshape(sources * block_len, HD)

    request = lax.axis_index("rq")
    positions = jnp.arange(sources * block_len, dtype=jnp.int32)
    within = positions % block_len
    source_row = positions // block_len
    text_pos = source_row * text_rows + within - patches
    live_text = text_pos < lax.dynamic_index_in_dim(txt_len, request, keepdims=False)
    allowed = (within < patches) | live_text

    attended = attend_one(head_queries, keys, values, allowed).reshape(sources, patches, HD)
    attended = lax.all_to_all(attended, ROW, 0, 0, tiled=True)
    attended = jnp.transpose(
        attended.reshape(requests, heads_local, patches, HD), (0, 2, 1, 3)
    ).reshape(requests * patches, cols_local)

    partial_value = lax.dot_general(
        attended,
        weight_t,
        (((1,), (1,)), ((), ())),
        preferred_element_type=jnp.float32,
    )
    slab_width = img_hidden.shape[2]
    col_index = lax.axis_index("col")
    shared_sum = lax.psum_scatter(partial_value, "col", scatter_dimension=1, tiled=True)
    col_mods = lax.dynamic_slice_in_dim(img_mod, col_index * slab_width, slab_width, 2)
    mixed = img_hidden.astype(jnp.float32) + col_mods[:, 2:3, :] * shared_sum.reshape(
        requests, patches, slab_width
    )
    row_sums, squares = lax.psum((jnp.sum(mixed, -1), jnp.sum(mixed * mixed, -1)), "col")
    row_mean = row_sums / D
    spread = squares / D - row_mean * row_mean
    scaled = (mixed - row_mean[..., None]) * lax.rsqrt(spread[..., None] + eps_norm)
    modulated = (scaled * (1.0 + col_mods[:, 4:5, :]) + col_mods[:, 3:4, :]).astype(jnp.bfloat16)
    velocity = lax.psum(
        jnp.dot(
            modulated.reshape(requests * patches, slab_width),
            final_weight,
            preferred_element_type=jnp.float32,
        ),
        "col",
    )
    velocity = velocity.reshape(requests, patches, latent.shape[2])
    sigma_now = sigma_at(step_idx)[:, None, None]
    sigma_next = sigma_at(step_idx - 1)[:, None, None]
    advanced = latent + (sigma_next - sigma_now) * velocity
    denoised = latent - sigma_now * velocity
    return (advanced, denoised)


def solution(mesh):
    rows = mesh.shape["row"]
    cols = mesh.shape["col"]
    split = Mesh(mesh.devices.reshape(REQ, rows // REQ, cols), ("rq", "rm", "col"))
    in_specs = (
        P(None, ROW, "col"),
        P(None, ROW, "col"),
        P(None, ROW, None),
        P(),
        P(),
        P(None, None, "col"),
        P(None, None, "col"),
        P("col", ROW),
        P("col", None),
        P(),
        P(),
        P(),
    )
    out_specs = (P(None, ROW, None), P(None, ROW, None))
    return jax.shard_map(
        per_device, mesh=split, in_specs=in_specs, out_specs=out_specs, check_vma=False
    )
```

```python
import jax
import jax.numpy as jnp
from jax import lax
from jax.sharding import Mesh
from jax.sharding import PartitionSpec as P

D = 2432
HD = 64
STEPS = 28
REQ = 8

ROW = ("rq", "rm")

eps_norm = 1e-06
neg_fill = -1e30


def layer_norm(values):
    average = jnp.mean(values, -1, keepdims=True)
    centred = values - average
    variance = jnp.mean(centred * centred, -1, keepdims=True)
    return centred * lax.rsqrt(variance + eps_norm)


def rms_heads(values, scaling):
    reshaped = values.reshape(values.shape[:-1] + (values.shape[-1] // HD, HD))
    inverse = lax.rsqrt(jnp.mean(reshaped * reshaped, -1, keepdims=True) + eps_norm)
    return (reshaped * inverse * scaling).astype(jnp.bfloat16)


def sigma_at(indices):
    fraction = indices.astype(jnp.float32) / STEPS
    return 3.0 * fraction / (1.0 + 2.0 * fraction)


def gather_features(local):
    stacked = lax.all_gather(local, "col", axis=0, tiled=False)
    slabs = stacked.shape[0]
    moved = jnp.moveaxis(stacked, 0, -2)
    return moved.reshape(local.shape[:-1] + (slabs * local.shape[-1],))


def attend_one(queries, keys, values, allowed):
    scores = jnp.dot(queries, keys.T, preferred_element_type=jnp.float32) * HD ** (-0.5)
    scores = jnp.where(allowed[None, :], scores, neg_fill)
    top_score = jnp.max(scores, -1, keepdims=True)
    exp_scores = jnp.where(allowed[None, :], jnp.exp(scores - top_score), 0.0)
    row_total = jnp.sum(exp_scores, -1, keepdims=True)
    weighted = jnp.dot(exp_scores.astype(jnp.bfloat16), values, preferred_element_type=jnp.float32)
    return (weighted / row_total).astype(jnp.bfloat16)


def per_device(
    img_hidden,
    txt_hidden,
    latent,
    img_mod,
    txt_mod,
    qkv_weight,
    txt_kv_weight,
    out_weight,
    final_weight,
    qk_gains,
    txt_len,
    step_idx,
):
    requests = img_hidden.shape[0]
    patches = img_hidden.shape[1]
    text_rows = txt_hidden.shape[1]
    cols_local = qkv_weight.shape[2]
    heads_local = cols_local // HD
    block_len = patches + text_rows

    weight_t = lax.all_gather(jnp.transpose(out_weight), ROW, axis=0, tiled=True)

    full_final = lax.all_gather(final_weight, "col", axis=0, tiled=True)
    img_full = gather_features(img_hidden)
    txt_full = gather_features(txt_hidden)
    img_wide = img_full.astype(jnp.float32)
    normed = (layer_norm(img_wide) * (1.0 + img_mod[:, 1:2, :]) + img_mod[:, 0:1, :]).astype(
        jnp.bfloat16
    )
    flat_rows = normed.reshape(requests * patches, D)
    projected = jnp.einsum("td,cde->cte", flat_rows, qkv_weight, preferred_element_type=jnp.float32)
    queries = rms_heads(projected[0], qk_gains[0]).reshape(requests, patches, cols_local)
    img_keys = rms_heads(projected[1], qk_gains[1]).reshape(requests, patches, cols_local)
    img_values = projected[2].astype(jnp.bfloat16).reshape(requests, patches, cols_local)
    text_normed = (
        layer_norm(txt_full.astype(jnp.float32)) * (1.0 + txt_mod[:, 1:2, :]) + txt_mod[:, 0:1, :]
    ).astype(jnp.bfloat16)
    text_proj = jnp.einsum(
        "rtd,cde->crte", text_normed, txt_kv_weight, preferred_element_type=jnp.float32
    )
    text_keys = rms_heads(text_proj[0], qk_gains[2]).reshape(requests, text_rows, cols_local)
    text_values = text_proj[1].astype(jnp.bfloat16)
    key_rows = jnp.concatenate([img_keys, text_keys], 1)
    value_rows = jnp.concatenate([img_values, text_values], 1)

    def by_head(values, length):
        split = values.reshape(requests, length, heads_local, HD)
        return jnp.transpose(split, (0, 2, 1, 3)).reshape(requests * heads_local, length, HD)

    bundle = jnp.concatenate(
        [by_head(queries, patches), by_head(key_rows, block_len), by_head(value_rows, block_len)], 1
    )
    bundle = lax.all_to_all(bundle, ROW, 0, 0, tiled=True)
    sources = bundle.shape[0]
    head_queries = bundle[:, :patches].reshape(sources * patches, HD)
    keys = bundle[:, patches : patches + block_len].reshape(sources * block_len, HD)
    values = bundle[:, patches + block_len :].reshape(sources * block_len, HD)

    request = lax.axis_index("rq")
    positions = jnp.arange(sources * block_len, dtype=jnp.int32)
    within = positions % block_len
    source_row = positions // block_len
    text_pos = source_row * text_rows + within - patches
    live_text = text_pos < lax.dynamic_index_in_dim(txt_len, request, keepdims=False)
    allowed = (within < patches) | live_text

    attended = attend_one(head_queries, keys, values, allowed).reshape(sources, patches, HD)
    attended = lax.all_to_all(attended, ROW, 0, 0, tiled=True)
    attended = jnp.transpose(
        attended.reshape(requests, heads_local, patches, HD), (0, 2, 1, 3)
    ).reshape(requests * patches, cols_local)

    partial_value = lax.dot_general(
        attended,
        weight_t,
        (((1,), (1,)), ((), ())),
        preferred_element_type=jnp.float32,
    )
    cols = lax.axis_size("col")
    col_index = lax.axis_index("col")
    shared_sum = lax.psum_scatter(partial_value, "col", scatter_dimension=0, tiled=True)
    own_requests = requests // cols
    first = col_index * own_requests
    own_mods = lax.dynamic_slice_in_dim(img_mod, first, own_requests, 0)
    own_hidden = lax.dynamic_slice_in_dim(img_wide, first, own_requests, 0)
    mixed = own_hidden + own_mods[:, 2:3, :] * shared_sum.reshape(own_requests, patches, D)
    modulated = (layer_norm(mixed) * (1.0 + own_mods[:, 4:5, :]) + own_mods[:, 3:4, :]).astype(
        jnp.bfloat16
    )
    velocity = jnp.dot(
        modulated.reshape(own_requests * patches, D),
        full_final,
        preferred_element_type=jnp.float32,
    ).reshape(own_requests, patches, latent.shape[2])
    own_latent = lax.dynamic_slice_in_dim(latent, first, own_requests, 0)
    own_steps = lax.dynamic_slice_in_dim(step_idx, first, own_requests, 0)
    sigma_now = sigma_at(own_steps)[:, None, None]
    sigma_next = sigma_at(own_steps - 1)[:, None, None]
    advanced = own_latent + (sigma_next - sigma_now) * velocity
    denoised = own_latent - sigma_now * velocity
    both = lax.all_gather(jnp.stack([advanced, denoised]), "col", axis=1, tiled=True)
    advanced, denoised = both[0], both[1]
    return (advanced, denoised)


def solution(mesh):
    rows = mesh.shape["row"]
    cols = mesh.shape["col"]
    split = Mesh(mesh.devices.reshape(REQ, rows // REQ, cols), ("rq", "rm", "col"))
    in_specs = (
        P(None, ROW, "col"),
        P(None, ROW, "col"),
        P(None, ROW, None),
        P(),
        P(),
        P(None, None, "col"),
        P(None, None, "col"),
        P("col", ROW),
        P("col", None),
        P(),
        P(),
        P(),
    )
    out_specs = (P(None, ROW, None), P(None, ROW, None))
    return jax.shard_map(
        per_device, mesh=split, in_specs=in_specs, out_specs=out_specs, check_vma=False
    )
```

```python
import jax
import jax.numpy as jnp
from jax import lax
from jax.sharding import Mesh
from jax.sharding import PartitionSpec as P

D = 2432
HD = 64
STEPS = 28
REQ = 8

ROW = ("rq", "rm")

eps_norm = 1e-06
neg_fill = -1e30


def layer_norm(values):
    average = jnp.mean(values, -1, keepdims=True)
    centred = values - average
    variance = jnp.mean(centred * centred, -1, keepdims=True)
    return centred * lax.rsqrt(variance + eps_norm)


def rms_heads(values, scaling):
    reshaped = values.reshape(values.shape[:-1] + (values.shape[-1] // HD, HD))
    inverse = lax.rsqrt(jnp.mean(reshaped * reshaped, -1, keepdims=True) + eps_norm)
    return (reshaped * inverse * scaling).astype(jnp.bfloat16)


def sigma_at(indices):
    fraction = indices.astype(jnp.float32) / STEPS
    return 3.0 * fraction / (1.0 + 2.0 * fraction)


def attend_one(queries, keys, values, allowed):
    scores = jnp.dot(queries, keys.T, preferred_element_type=jnp.float32) * HD ** (-0.5)
    scores = jnp.where(allowed[None, :], scores, neg_fill)
    top_score = jnp.max(scores, -1, keepdims=True)
    exp_scores = jnp.where(allowed[None, :], jnp.exp(scores - top_score), 0.0)
    row_total = jnp.sum(exp_scores, -1, keepdims=True)
    weighted = jnp.dot(exp_scores.astype(jnp.bfloat16), values, preferred_element_type=jnp.float32)
    return (weighted / row_total).astype(jnp.bfloat16)


def per_device(
    img_hidden,
    txt_hidden,
    latent,
    img_mod,
    txt_mod,
    qkv_weight,
    txt_kv_weight,
    out_weight,
    final_weight,
    qk_gains,
    txt_len,
    step_idx,
):
    requests = img_hidden.shape[0]
    patches = img_hidden.shape[1]
    text_rows = txt_hidden.shape[1]
    cols_local = qkv_weight.shape[2]
    heads_local = cols_local // HD
    block_len = patches + text_rows

    weight_t = lax.all_gather(jnp.transpose(out_weight), ROW, axis=0, tiled=True)

    img_rows = img_hidden.reshape(requests * patches, -1)
    txt_rows = txt_hidden.reshape(requests * text_rows, -1)
    packed = jnp.concatenate([img_rows, txt_rows, jnp.transpose(final_weight)], 0)
    packed = lax.all_gather(packed, "col", axis=0, tiled=False)
    slabs = packed.shape[0]

    def joined(part):
        return jnp.moveaxis(part, 0, -2).reshape(part.shape[1], slabs * part.shape[2])

    img_count = requests * patches
    txt_count = requests * text_rows
    img_full = joined(packed[:, :img_count]).reshape(requests, patches, D)
    txt_full = joined(packed[:, img_count : img_count + txt_count]).reshape(requests, text_rows, D)
    final_slabs = packed[:, img_count + txt_count :]
    img_wide = img_full.astype(jnp.float32)
    normed = (layer_norm(img_wide) * (1.0 + img_mod[:, 1:2, :]) + img_mod[:, 0:1, :]).astype(
        jnp.bfloat16
    )
    flat_rows = normed.reshape(requests * patches, D)
    projected = jnp.einsum("td,cde->cte", flat_rows, qkv_weight, preferred_element_type=jnp.float32)
    queries = rms_heads(projected[0], qk_gains[0]).reshape(requests, patches, cols_local)
    img_keys = rms_heads(projected[1], qk_gains[1]).reshape(requests, patches, cols_local)
    img_values = projected[2].astype(jnp.bfloat16).reshape(requests, patches, cols_local)
    text_normed = (
        layer_norm(txt_full.astype(jnp.float32)) * (1.0 + txt_mod[:, 1:2, :]) + txt_mod[:, 0:1, :]
    ).astype(jnp.bfloat16)
    text_proj = jnp.einsum(
        "rtd,cde->crte", text_normed, txt_kv_weight, preferred_element_type=jnp.float32
    )
    text_keys = rms_heads(text_proj[0], qk_gains[2]).reshape(requests, text_rows, cols_local)
    text_values = text_proj[1].astype(jnp.bfloat16)
    key_rows = jnp.concatenate([img_keys, text_keys], 1)
    value_rows = jnp.concatenate([img_values, text_values], 1)

    def by_head(values, length):
        split = values.reshape(requests, length, heads_local, HD)
        return jnp.transpose(split, (0, 2, 1, 3)).reshape(requests * heads_local, length, HD)

    head_queries = lax.all_to_all(by_head(queries, patches), ROW, 0, 0, tiled=True)
    bundle = jnp.concatenate([by_head(key_rows, block_len), by_head(value_rows, block_len)], 1)
    bundle = lax.all_to_all(bundle, ROW, 0, 0, tiled=True)
    sources = bundle.shape[0]
    head_queries = head_queries.reshape(sources * patches, HD)
    keys = bundle[:, :block_len].reshape(sources * block_len, HD)
    values = bundle[:, block_len:].reshape(sources * block_len, HD)

    request = lax.axis_index("rq")
    positions = jnp.arange(sources * block_len, dtype=jnp.int32)
    within = positions % block_len
    source_row = positions // block_len
    text_pos = source_row * text_rows + within - patches
    live_text = text_pos < lax.dynamic_index_in_dim(txt_len, request, keepdims=False)
    allowed = (within < patches) | live_text

    attended = attend_one(head_queries, keys, values, allowed).reshape(sources, patches, HD)
    attended = lax.all_to_all(attended, ROW, 0, 0, tiled=True)
    attended = jnp.transpose(
        attended.reshape(requests, heads_local, patches, HD), (0, 2, 1, 3)
    ).reshape(requests * patches, cols_local)

    partial_value = lax.dot_general(
        attended,
        weight_t,
        (((1,), (1,)), ((), ())),
        preferred_element_type=jnp.float32,
    )
    cols = lax.axis_size("col")
    col_index = lax.axis_index("col")
    shared_sum = lax.psum_scatter(partial_value, "col", scatter_dimension=0, tiled=True)
    own_requests = requests // cols
    first = col_index * own_requests
    own_mods = lax.dynamic_slice_in_dim(img_mod, first, own_requests, 0)
    own_hidden = lax.dynamic_slice_in_dim(img_wide, first, own_requests, 0)
    mixed = own_hidden + own_mods[:, 2:3, :] * shared_sum.reshape(own_requests, patches, D)
    modulated = (layer_norm(mixed) * (1.0 + own_mods[:, 4:5, :]) + own_mods[:, 3:4, :]).astype(
        jnp.bfloat16
    )
    velocity = jnp.einsum(
        "tcf,cof->to",
        modulated.reshape(own_requests * patches, slabs, D // slabs),
        final_slabs,
        preferred_element_type=jnp.float32,
    ).reshape(own_requests, patches, latent.shape[2])
    own_latent = lax.dynamic_slice_in_dim(latent, first, own_requests, 0)
    own_steps = lax.dynamic_slice_in_dim(step_idx, first, own_requests, 0)
    sigma_now = sigma_at(own_steps)[:, None, None]
    sigma_next = sigma_at(own_steps - 1)[:, None, None]
    advanced = own_latent + (sigma_next - sigma_now) * velocity
    denoised = own_latent - sigma_now * velocity
    both = lax.all_gather(jnp.stack([advanced, denoised]), "col", axis=1, tiled=True)
    advanced, denoised = both[0], both[1]
    return (advanced, denoised)


def solution(mesh):
    rows = mesh.shape["row"]
    cols = mesh.shape["col"]
    split = Mesh(mesh.devices.reshape(REQ, rows // REQ, cols), ("rq", "rm", "col"))
    in_specs = (
        P(None, ROW, "col"),
        P(None, ROW, "col"),
        P(None, ROW, None),
        P(),
        P(),
        P(None, None, "col"),
        P(None, None, "col"),
        P("col", ROW),
        P("col", None),
        P(),
        P(),
        P(),
    )
    out_specs = (P(None, ROW, None), P(None, ROW, None))
    return jax.shard_map(
        per_device, mesh=split, in_specs=in_specs, out_specs=out_specs, check_vma=False
    )
```

```python
import jax
import jax.numpy as jnp
from jax import lax
from jax.sharding import Mesh
from jax.sharding import PartitionSpec as P

D = 2432
HD = 64
STEPS = 28
REQ = 8

ROW = ("rq", "rm")

eps_norm = 1e-06
neg_fill = -1e30


def layer_norm(values):
    average = jnp.mean(values, -1, keepdims=True)
    centred = values - average
    variance = jnp.mean(centred * centred, -1, keepdims=True)
    return centred * lax.rsqrt(variance + eps_norm)


def rms_heads(values, scaling):
    reshaped = values.reshape(values.shape[:-1] + (values.shape[-1] // HD, HD))
    inverse = lax.rsqrt(jnp.mean(reshaped * reshaped, -1, keepdims=True) + eps_norm)
    return (reshaped * inverse * scaling).astype(jnp.bfloat16)


def sigma_at(indices):
    fraction = indices.astype(jnp.float32) / STEPS
    return 3.0 * fraction / (1.0 + 2.0 * fraction)


def gather_features(local):
    stacked = lax.all_gather(local, "col", axis=0, tiled=False)
    slabs = stacked.shape[0]
    moved = jnp.moveaxis(stacked, 0, -2)
    return moved.reshape(local.shape[:-1] + (slabs * local.shape[-1],))


def attend_one(queries, keys, values, allowed):
    scores = jnp.dot(queries, keys.T, preferred_element_type=jnp.float32) * HD ** (-0.5)
    scores = jnp.where(allowed[None, :], scores, neg_fill)
    top_score = jnp.max(scores, -1, keepdims=True)
    exp_scores = jnp.where(allowed[None, :], jnp.exp(scores - top_score), 0.0)
    row_total = jnp.sum(exp_scores, -1, keepdims=True)
    weighted = jnp.dot(exp_scores.astype(jnp.bfloat16), values, preferred_element_type=jnp.float32)
    return (weighted / row_total).astype(jnp.bfloat16)


def per_device(
    img_hidden,
    txt_hidden,
    latent,
    img_mod,
    txt_mod,
    qkv_weight,
    txt_kv_weight,
    out_weight,
    final_weight,
    qk_gains,
    txt_len,
    step_idx,
):
    requests = img_hidden.shape[0]
    patches = img_hidden.shape[1]
    text_rows = txt_hidden.shape[1]
    cols_local = qkv_weight.shape[2]
    heads_local = cols_local // HD
    block_len = patches + text_rows

    weight_t = lax.all_gather(jnp.transpose(out_weight), ROW, axis=0, tiled=True)

    img_full = gather_features(img_hidden)
    txt_rows = txt_hidden.reshape(requests * text_rows, -1)
    packed = jnp.concatenate([txt_rows, jnp.transpose(final_weight)], 0)
    packed = lax.all_gather(packed, "col", axis=0, tiled=False)
    slabs = packed.shape[0]
    txt_count = requests * text_rows
    txt_full = (
        jnp.moveaxis(packed[:, :txt_count], 0, -2)
        .reshape(txt_count, D)
        .reshape(requests, text_rows, D)
    )
    final_slabs = packed[:, txt_count:]
    normed = (layer_norm(img_full.astype(jnp.float32)) * (1.0 + img_mod[:, 1:2, :]) + img_mod[:, 0:1, :]).astype(
        jnp.bfloat16
    )
    flat_rows = normed.reshape(requests * patches, D)
    projected = jnp.einsum("td,cde->cte", flat_rows, qkv_weight, preferred_element_type=jnp.float32)
    queries = rms_heads(projected[0], qk_gains[0]).reshape(requests, patches, cols_local)
    img_keys = rms_heads(projected[1], qk_gains[1]).reshape(requests, patches, cols_local)
    img_values = projected[2].astype(jnp.bfloat16).reshape(requests, patches, cols_local)
    text_normed = (
        layer_norm(txt_full.astype(jnp.float32)) * (1.0 + txt_mod[:, 1:2, :]) + txt_mod[:, 0:1, :]
    ).astype(jnp.bfloat16)
    text_proj = jnp.einsum(
        "rtd,cde->crte", text_normed, txt_kv_weight, preferred_element_type=jnp.float32
    )
    text_keys = rms_heads(text_proj[0], qk_gains[2]).reshape(requests, text_rows, cols_local)
    text_values = text_proj[1].astype(jnp.bfloat16)
    key_rows = jnp.concatenate([img_keys, text_keys], 1)
    value_rows = jnp.concatenate([img_values, text_values], 1)

    def by_head(values, length):
        split = values.reshape(requests, length, heads_local, HD)
        return jnp.transpose(split, (0, 2, 1, 3)).reshape(requests * heads_local, length, HD)

    bundle = jnp.concatenate(
        [by_head(queries, patches), by_head(key_rows, block_len), by_head(value_rows, block_len)], 1
    )
    bundle = lax.all_to_all(bundle, ROW, 0, 0, tiled=True)
    sources = bundle.shape[0]
    head_queries = bundle[:, :patches].reshape(sources * patches, HD)
    keys = bundle[:, patches : patches + block_len].reshape(sources * block_len, HD)
    values = bundle[:, patches + block_len :].reshape(sources * block_len, HD)

    request = lax.axis_index("rq")
    positions = jnp.arange(sources * block_len, dtype=jnp.int32)
    within = positions % block_len
    source_row = positions // block_len
    text_pos = source_row * text_rows + within - patches
    live_text = text_pos < lax.dynamic_index_in_dim(txt_len, request, keepdims=False)
    allowed = (within < patches) | live_text

    attended = attend_one(head_queries, keys, values, allowed).reshape(sources, patches, HD)
    attended = lax.all_to_all(attended, ROW, 0, 0, tiled=True)
    attended = jnp.transpose(
        attended.reshape(requests, heads_local, patches, HD), (0, 2, 1, 3)
    ).reshape(requests * patches, cols_local)

    partial_value = lax.dot_general(
        attended,
        weight_t,
        (((1,), (1,)), ((), ())),
        preferred_element_type=jnp.float32,
    )
    cols = lax.axis_size("col")
    col_index = lax.axis_index("col")
    shared_sum = lax.psum_scatter(partial_value, "col", scatter_dimension=0, tiled=True)
    own_requests = requests // cols
    first = col_index * own_requests
    own_mods = lax.dynamic_slice_in_dim(img_mod, first, own_requests, 0)
    own_hidden = lax.dynamic_slice_in_dim(img_full, first, own_requests, 0).astype(jnp.float32)
    mixed = own_hidden + own_mods[:, 2:3, :] * shared_sum.reshape(own_requests, patches, D)
    modulated = (layer_norm(mixed) * (1.0 + own_mods[:, 4:5, :]) + own_mods[:, 3:4, :]).astype(
        jnp.bfloat16
    )
    velocity = jnp.einsum(
        "tcf,cof->to",
        modulated.reshape(own_requests * patches, slabs, D // slabs),
        final_slabs,
        preferred_element_type=jnp.float32,
    ).reshape(own_requests, patches, latent.shape[2])
    own_latent = lax.dynamic_slice_in_dim(latent, first, own_requests, 0)
    own_steps = lax.dynamic_slice_in_dim(step_idx, first, own_requests, 0)
    sigma_now = sigma_at(own_steps)[:, None, None]
    sigma_next = sigma_at(own_steps - 1)[:, None, None]
    advanced = own_latent + (sigma_next - sigma_now) * velocity
    denoised = own_latent - sigma_now * velocity
    both = lax.all_gather(jnp.stack([advanced, denoised]), "col", axis=1, tiled=True)
    advanced, denoised = both[0], both[1]
    return (advanced, denoised)


def solution(mesh):
    rows = mesh.shape["row"]
    cols = mesh.shape["col"]
    split = Mesh(mesh.devices.reshape(REQ, rows // REQ, cols), ("rq", "rm", "col"))
    in_specs = (
        P(None, ROW, "col"),
        P(None, ROW, "col"),
        P(None, ROW, None),
        P(),
        P(),
        P(None, None, "col"),
        P(None, None, "col"),
        P("col", ROW),
        P("col", None),
        P(),
        P(),
        P(),
    )
    out_specs = (P(None, ROW, None), P(None, ROW, None))
    return jax.shard_map(
        per_device, mesh=split, in_specs=in_specs, out_specs=out_specs, check_vma=False
    )
```

```python
import jax
import jax.numpy as jnp
from jax import lax
from jax.sharding import Mesh
from jax.sharding import PartitionSpec as P

D = 2432
HD = 64
STEPS = 28
REQ = 8

ROW = ("rq", "rm")

eps_norm = 1e-06
neg_fill = -1e30


def layer_norm(values):
    average = jnp.mean(values, -1, keepdims=True)
    centred = values - average
    variance = jnp.mean(centred * centred, -1, keepdims=True)
    return centred * lax.rsqrt(variance + eps_norm)


def rms_heads(values, scaling):
    reshaped = values.reshape(values.shape[:-1] + (values.shape[-1] // HD, HD))
    inverse = lax.rsqrt(jnp.mean(reshaped * reshaped, -1, keepdims=True) + eps_norm)
    return (reshaped * inverse * scaling).astype(jnp.bfloat16)


def sigma_at(indices):
    fraction = indices.astype(jnp.float32) / STEPS
    return 3.0 * fraction / (1.0 + 2.0 * fraction)


def gather_features(local):
    stacked = lax.all_gather(local, "col", axis=0, tiled=False)
    slabs = stacked.shape[0]
    moved = jnp.moveaxis(stacked, 0, -2)
    return moved.reshape(local.shape[:-1] + (slabs * local.shape[-1],))


def attend_one(queries, keys, values, allowed):
    scores = jnp.dot(queries, keys.T, preferred_element_type=jnp.float32) * HD ** (-0.5)
    scores = jnp.where(allowed[None, :], scores, neg_fill)
    top_score = jnp.max(scores, -1, keepdims=True)
    exp_scores = jnp.where(allowed[None, :], jnp.exp(scores - top_score), 0.0)
    row_total = jnp.sum(exp_scores, -1, keepdims=True)
    weighted = jnp.dot(exp_scores.astype(jnp.bfloat16), values, preferred_element_type=jnp.float32)
    return (weighted / row_total).astype(jnp.bfloat16)


def per_device(
    img_hidden,
    txt_hidden,
    latent,
    img_mod,
    txt_mod,
    qkv_weight,
    txt_kv_weight,
    out_weight,
    final_weight,
    qk_gains,
    txt_len,
    step_idx,
):
    requests = img_hidden.shape[0]
    patches = img_hidden.shape[1]
    text_rows = txt_hidden.shape[1]
    cols_local = qkv_weight.shape[2]
    heads_local = cols_local // HD
    block_len = patches + text_rows

    weight_t = lax.all_gather(jnp.transpose(out_weight), ROW, axis=0, tiled=True)

    img_full = gather_features(img_hidden)
    txt_rows = txt_hidden.reshape(requests * text_rows, -1)
    packed = jnp.concatenate([txt_rows, jnp.transpose(final_weight)], 0)
    packed = lax.all_gather(packed, "col", axis=0, tiled=False)
    slabs = packed.shape[0]
    txt_count = requests * text_rows
    txt_full = (
        jnp.moveaxis(packed[:, :txt_count], 0, -2)
        .reshape(txt_count, D)
        .reshape(requests, text_rows, D)
    )
    final_slabs = packed[:, txt_count:]
    normed = (layer_norm(img_full.astype(jnp.float32)) * (1.0 + img_mod[:, 1:2, :]) + img_mod[:, 0:1, :]).astype(
        jnp.bfloat16
    )
    flat_rows = normed.reshape(requests * patches, D)
    projected = jnp.einsum("td,cde->cte", flat_rows, qkv_weight, preferred_element_type=jnp.float32)
    queries = rms_heads(projected[0], qk_gains[0]).reshape(requests, patches, cols_local)
    img_keys = rms_heads(projected[1], qk_gains[1]).reshape(requests, patches, cols_local)
    img_values = projected[2].astype(jnp.bfloat16).reshape(requests, patches, cols_local)
    text_normed = (
        layer_norm(txt_full.astype(jnp.float32)) * (1.0 + txt_mod[:, 1:2, :]) + txt_mod[:, 0:1, :]
    ).astype(jnp.bfloat16)
    text_proj = jnp.einsum(
        "rtd,cde->crte", text_normed, txt_kv_weight, preferred_element_type=jnp.float32
    )
    text_keys = rms_heads(text_proj[0], qk_gains[2]).reshape(requests, text_rows, cols_local)
    text_values = text_proj[1].astype(jnp.bfloat16)
    key_rows = jnp.concatenate([img_keys, text_keys], 1)
    value_rows = jnp.concatenate([img_values, text_values], 1)

    def by_head(values, length):
        split = values.reshape(requests, length, heads_local, HD)
        return jnp.transpose(split, (0, 2, 1, 3)).reshape(requests * heads_local, length, HD)

    bundle = jnp.concatenate(
        [by_head(queries, patches), by_head(key_rows, block_len), by_head(value_rows, block_len)], 1
    )
    sources, bundle_rows = bundle.shape[0], bundle.shape[1]
    bundle = bundle.reshape(sources, bundle_rows // 2, 2 * HD)
    bundle = lax.all_to_all(bundle, ROW, 0, 0, tiled=True)
    bundle = bundle.reshape(sources, bundle_rows, HD)
    head_queries = bundle[:, :patches].reshape(sources * patches, HD)
    keys = bundle[:, patches : patches + block_len].reshape(sources * block_len, HD)
    values = bundle[:, patches + block_len :].reshape(sources * block_len, HD)

    request = lax.axis_index("rq")
    positions = jnp.arange(sources * block_len, dtype=jnp.int32)
    within = positions % block_len
    source_row = positions // block_len
    text_pos = source_row * text_rows + within - patches
    live_text = text_pos < lax.dynamic_index_in_dim(txt_len, request, keepdims=False)
    allowed = (within < patches) | live_text

    attended = attend_one(head_queries, keys, values, allowed).reshape(sources, patches, HD)
    attended = lax.all_to_all(attended, ROW, 0, 0, tiled=True)
    attended = jnp.transpose(
        attended.reshape(requests, heads_local, patches, HD), (0, 2, 1, 3)
    ).reshape(requests * patches, cols_local)

    partial_value = lax.dot_general(
        attended,
        weight_t,
        (((1,), (1,)), ((), ())),
        preferred_element_type=jnp.float32,
    )
    cols = lax.axis_size("col")
    col_index = lax.axis_index("col")
    shared_sum = lax.psum_scatter(partial_value, "col", scatter_dimension=0, tiled=True)
    own_requests = requests // cols
    first = col_index * own_requests
    own_mods = lax.dynamic_slice_in_dim(img_mod, first, own_requests, 0)
    own_hidden = lax.dynamic_slice_in_dim(img_full, first, own_requests, 0).astype(jnp.float32)
    mixed = own_hidden + own_mods[:, 2:3, :] * shared_sum.reshape(own_requests, patches, D)
    modulated = (layer_norm(mixed) * (1.0 + own_mods[:, 4:5, :]) + own_mods[:, 3:4, :]).astype(
        jnp.bfloat16
    )
    velocity = jnp.einsum(
        "tcf,cof->to",
        modulated.reshape(own_requests * patches, slabs, D // slabs),
        final_slabs,
        preferred_element_type=jnp.float32,
    ).reshape(own_requests, patches, latent.shape[2])
    own_latent = lax.dynamic_slice_in_dim(latent, first, own_requests, 0)
    own_steps = lax.dynamic_slice_in_dim(step_idx, first, own_requests, 0)
    sigma_now = sigma_at(own_steps)[:, None, None]
    sigma_next = sigma_at(own_steps - 1)[:, None, None]
    advanced = own_latent + (sigma_next - sigma_now) * velocity
    denoised = own_latent - sigma_now * velocity
    both = lax.all_gather(jnp.stack([advanced, denoised]), "col", axis=1, tiled=True)
    advanced, denoised = both[0], both[1]
    return (advanced, denoised)


def solution(mesh):
    rows = mesh.shape["row"]
    cols = mesh.shape["col"]
    split = Mesh(mesh.devices.reshape(REQ, rows // REQ, cols), ("rq", "rm", "col"))
    in_specs = (
        P(None, ROW, "col"),
        P(None, ROW, "col"),
        P(None, ROW, None),
        P(),
        P(),
        P(None, None, "col"),
        P(None, None, "col"),
        P("col", ROW),
        P("col", None),
        P(),
        P(),
        P(),
    )
    out_specs = (P(None, ROW, None), P(None, ROW, None))
    return jax.shard_map(
        per_device, mesh=split, in_specs=in_specs, out_specs=out_specs, check_vma=False
    )
```

```python
import jax
import jax.numpy as jnp
from jax import lax
from jax.sharding import Mesh
from jax.sharding import PartitionSpec as P

D = 2432
HD = 64
STEPS = 28
REQ = 8

ROW = ("rq", "rm")

eps_norm = 1e-06
neg_fill = -1e30


def layer_norm(values):
    average = jnp.mean(values, -1, keepdims=True)
    centred = values - average
    variance = jnp.mean(centred * centred, -1, keepdims=True)
    return centred * lax.rsqrt(variance + eps_norm)


def rms_heads(values, scaling):
    reshaped = values.reshape(values.shape[:-1] + (values.shape[-1] // HD, HD))
    inverse = lax.rsqrt(jnp.mean(reshaped * reshaped, -1, keepdims=True) + eps_norm)
    return (reshaped * inverse * scaling).astype(jnp.bfloat16)


def sigma_at(indices):
    fraction = indices.astype(jnp.float32) / STEPS
    return 3.0 * fraction / (1.0 + 2.0 * fraction)


def gather_features(local):
    stacked = lax.all_gather(local, "col", axis=0, tiled=False)
    slabs = stacked.shape[0]
    moved = jnp.moveaxis(stacked, 0, -2)
    return moved.reshape(local.shape[:-1] + (slabs * local.shape[-1],))


def halving_scatter(partial, cols, col_index):
    rows = partial.shape[0] // cols
    chunks = partial.reshape((2, 2, rows) + partial.shape[1:])
    low = col_index % 2
    high = col_index // 2
    keep = lax.dynamic_index_in_dim(chunks, low, 1, keepdims=False)
    send = lax.dynamic_index_in_dim(chunks, 1 - low, 1, keepdims=False)
    pairs = [(i, i ^ 1) for i in range(cols)]
    halves = keep + lax.ppermute(send, "col", pairs)
    keep = lax.dynamic_index_in_dim(halves, high, 0, keepdims=False)
    send = lax.dynamic_index_in_dim(halves, 1 - high, 0, keepdims=False)
    pairs = [(i, i ^ 2) for i in range(cols)]
    return keep + lax.ppermute(send, "col", pairs)


def attend_one(queries, keys, values, allowed):
    scores = jnp.dot(queries, keys.T, preferred_element_type=jnp.float32) * HD ** (-0.5)
    scores = jnp.where(allowed[None, :], scores, neg_fill)
    top_score = jnp.max(scores, -1, keepdims=True)
    exp_scores = jnp.where(allowed[None, :], jnp.exp(scores - top_score), 0.0)
    row_total = jnp.sum(exp_scores, -1, keepdims=True)
    weighted = jnp.dot(exp_scores.astype(jnp.bfloat16), values, preferred_element_type=jnp.float32)
    return (weighted / row_total).astype(jnp.bfloat16)


def per_device(
    img_hidden,
    txt_hidden,
    latent,
    img_mod,
    txt_mod,
    qkv_weight,
    txt_kv_weight,
    out_weight,
    final_weight,
    qk_gains,
    txt_len,
    step_idx,
):
    requests = img_hidden.shape[0]
    patches = img_hidden.shape[1]
    text_rows = txt_hidden.shape[1]
    cols_local = qkv_weight.shape[2]
    heads_local = cols_local // HD
    block_len = patches + text_rows

    weight_t = lax.all_gather(jnp.transpose(out_weight), ROW, axis=0, tiled=True)

    img_full = gather_features(img_hidden)
    txt_rows = txt_hidden.reshape(requests * text_rows, -1)
    packed = jnp.concatenate([txt_rows, jnp.transpose(final_weight)], 0)
    packed = lax.all_gather(packed, "col", axis=0, tiled=False)
    slabs = packed.shape[0]
    txt_count = requests * text_rows
    txt_full = (
        jnp.moveaxis(packed[:, :txt_count], 0, -2)
        .reshape(txt_count, D)
        .reshape(requests, text_rows, D)
    )
    final_slabs = packed[:, txt_count:]
    normed = (layer_norm(img_full.astype(jnp.float32)) * (1.0 + img_mod[:, 1:2, :]) + img_mod[:, 0:1, :]).astype(
        jnp.bfloat16
    )
    flat_rows = normed.reshape(requests * patches, D)
    projected = jnp.einsum("td,cde->cte", flat_rows, qkv_weight, preferred_element_type=jnp.float32)
    queries = rms_heads(projected[0], qk_gains[0]).reshape(requests, patches, cols_local)
    img_keys = rms_heads(projected[1], qk_gains[1]).reshape(requests, patches, cols_local)
    img_values = projected[2].astype(jnp.bfloat16).reshape(requests, patches, cols_local)
    text_normed = (
        layer_norm(txt_full.astype(jnp.float32)) * (1.0 + txt_mod[:, 1:2, :]) + txt_mod[:, 0:1, :]
    ).astype(jnp.bfloat16)
    text_proj = jnp.einsum(
        "rtd,cde->crte", text_normed, txt_kv_weight, preferred_element_type=jnp.float32
    )
    text_keys = rms_heads(text_proj[0], qk_gains[2]).reshape(requests, text_rows, cols_local)
    text_values = text_proj[1].astype(jnp.bfloat16)
    key_rows = jnp.concatenate([img_keys, text_keys], 1)
    value_rows = jnp.concatenate([img_values, text_values], 1)

    def by_head(values, length):
        split = values.reshape(requests, length, heads_local, HD)
        return jnp.transpose(split, (0, 2, 1, 3)).reshape(requests * heads_local, length, HD)

    bundle = jnp.concatenate(
        [by_head(queries, patches), by_head(key_rows, block_len), by_head(value_rows, block_len)], 1
    )
    sources, bundle_rows = bundle.shape[0], bundle.shape[1]
    bundle = bundle.reshape(sources, bundle_rows // 2, 2 * HD)
    bundle = lax.all_to_all(bundle, ROW, 0, 0, tiled=True)
    bundle = bundle.reshape(sources, bundle_rows, HD)
    head_queries = bundle[:, :patches].reshape(sources * patches, HD)
    keys = bundle[:, patches : patches + block_len].reshape(sources * block_len, HD)
    values = bundle[:, patches + block_len :].reshape(sources * block_len, HD)

    request = lax.axis_index("rq")
    positions = jnp.arange(sources * block_len, dtype=jnp.int32)
    within = positions % block_len
    source_row = positions // block_len
    text_pos = source_row * text_rows + within - patches
    live_text = text_pos < lax.dynamic_index_in_dim(txt_len, request, keepdims=False)
    allowed = (within < patches) | live_text

    attended = attend_one(head_queries, keys, values, allowed).reshape(sources, patches, HD)
    attended = lax.all_to_all(attended, ROW, 0, 0, tiled=True)
    attended = jnp.transpose(
        attended.reshape(requests, heads_local, patches, HD), (0, 2, 1, 3)
    ).reshape(requests * patches, cols_local)

    partial_value = lax.dot_general(
        attended,
        weight_t,
        (((1,), (1,)), ((), ())),
        preferred_element_type=jnp.float32,
    )
    cols = lax.axis_size("col")
    col_index = lax.axis_index("col")
    shared_sum = halving_scatter(partial_value, cols, col_index)
    own_requests = requests // cols
    first = col_index * own_requests
    own_mods = lax.dynamic_slice_in_dim(img_mod, first, own_requests, 0)
    own_hidden = lax.dynamic_slice_in_dim(img_full, first, own_requests, 0).astype(jnp.float32)
    mixed = own_hidden + own_mods[:, 2:3, :] * shared_sum.reshape(own_requests, patches, D)
    modulated = (layer_norm(mixed) * (1.0 + own_mods[:, 4:5, :]) + own_mods[:, 3:4, :]).astype(
        jnp.bfloat16
    )
    velocity = jnp.einsum(
        "tcf,cof->to",
        modulated.reshape(own_requests * patches, slabs, D // slabs),
        final_slabs,
        preferred_element_type=jnp.float32,
    ).reshape(own_requests, patches, latent.shape[2])
    own_latent = lax.dynamic_slice_in_dim(latent, first, own_requests, 0)
    own_steps = lax.dynamic_slice_in_dim(step_idx, first, own_requests, 0)
    sigma_now = sigma_at(own_steps)[:, None, None]
    sigma_next = sigma_at(own_steps - 1)[:, None, None]
    advanced = own_latent + (sigma_next - sigma_now) * velocity
    denoised = own_latent - sigma_now * velocity
    both = lax.all_gather(jnp.stack([advanced, denoised]), "col", axis=1, tiled=True)
    advanced, denoised = both[0], both[1]
    return (advanced, denoised)


def solution(mesh):
    rows = mesh.shape["row"]
    cols = mesh.shape["col"]
    split = Mesh(mesh.devices.reshape(REQ, rows // REQ, cols), ("rq", "rm", "col"))
    in_specs = (
        P(None, ROW, "col"),
        P(None, ROW, "col"),
        P(None, ROW, None),
        P(),
        P(),
        P(None, None, "col"),
        P(None, None, "col"),
        P("col", ROW),
        P("col", None),
        P(),
        P(),
        P(),
    )
    out_specs = (P(None, ROW, None), P(None, ROW, None))
    return jax.shard_map(
        per_device, mesh=split, in_specs=in_specs, out_specs=out_specs, check_vma=False
    )
```

```python
import jax
import jax.numpy as jnp
from jax import lax
from jax.sharding import Mesh
from jax.sharding import PartitionSpec as P

D = 2432
HD = 64
STEPS = 28
REQ = 8

ROW = ("rq", "rm")

eps_norm = 1e-06
neg_fill = -1e30


def layer_norm(values):
    average = jnp.mean(values, -1, keepdims=True)
    centred = values - average
    variance = jnp.mean(centred * centred, -1, keepdims=True)
    return centred * lax.rsqrt(variance + eps_norm)


def rms_heads(values, scaling):
    reshaped = values.reshape(values.shape[:-1] + (values.shape[-1] // HD, HD))
    inverse = lax.rsqrt(jnp.mean(reshaped * reshaped, -1, keepdims=True) + eps_norm)
    return (reshaped * inverse * scaling).astype(jnp.bfloat16)


def sigma_at(indices):
    fraction = indices.astype(jnp.float32) / STEPS
    return 3.0 * fraction / (1.0 + 2.0 * fraction)


def gather_features(local):
    stacked = lax.all_gather(local, "col", axis=0, tiled=False)
    slabs = stacked.shape[0]
    moved = jnp.moveaxis(stacked, 0, -2)
    return moved.reshape(local.shape[:-1] + (slabs * local.shape[-1],))


def halving_scatter(partial, cols, col_index):
    rows = partial.shape[0] // cols
    chunks = partial.reshape((2, 2, rows) + partial.shape[1:])
    low = col_index % 2
    high = col_index // 2
    keep = lax.dynamic_index_in_dim(chunks, low, 1, keepdims=False)
    send = lax.dynamic_index_in_dim(chunks, 1 - low, 1, keepdims=False)
    pairs = [(i, i ^ 1) for i in range(cols)]
    halves = keep + lax.ppermute(send, "col", pairs)
    keep = lax.dynamic_index_in_dim(halves, high, 0, keepdims=False)
    send = lax.dynamic_index_in_dim(halves, 1 - high, 0, keepdims=False)
    pairs = [(i, i ^ 2) for i in range(cols)]
    return keep + lax.ppermute(send, "col", pairs)


def doubling_gather(block):
    rows = lax.axis_size(ROW)
    index = lax.axis_index(ROW)
    bits = rows.bit_length() - 1
    order = [3, 2, 5, 1, 4, 0][:bits] if bits == 6 else list(range(bits))
    buffer = block[None]
    for bit in order:
        pairs = [(i, i ^ (1 << bit)) for i in range(rows)]
        received = lax.ppermute(buffer, ROW, pairs)
        upper = (index >> bit) % 2 == 1
        buffer = jnp.where(
            upper,
            jnp.stack([received, buffer]),
            jnp.stack([buffer, received]),
        )
    done = list(reversed(order))
    buffer = buffer.reshape((2,) * bits + block.shape)
    perm = [done.index(bit) for bit in reversed(range(bits))]
    buffer = jnp.transpose(buffer, perm + [bits, bits + 1])
    return buffer.reshape((rows * block.shape[0],) + block.shape[1:])


def attend_one(queries, keys, values, allowed):
    scores = jnp.dot(queries, keys.T, preferred_element_type=jnp.float32) * HD ** (-0.5)
    scores = jnp.where(allowed[None, :], scores, neg_fill)
    top_score = jnp.max(scores, -1, keepdims=True)
    exp_scores = jnp.where(allowed[None, :], jnp.exp(scores - top_score), 0.0)
    row_total = jnp.sum(exp_scores, -1, keepdims=True)
    weighted = jnp.dot(exp_scores.astype(jnp.bfloat16), values, preferred_element_type=jnp.float32)
    return (weighted / row_total).astype(jnp.bfloat16)


def per_device(
    img_hidden,
    txt_hidden,
    latent,
    img_mod,
    txt_mod,
    qkv_weight,
    txt_kv_weight,
    out_weight,
    final_weight,
    qk_gains,
    txt_len,
    step_idx,
):
    requests = img_hidden.shape[0]
    patches = img_hidden.shape[1]
    text_rows = txt_hidden.shape[1]
    cols_local = qkv_weight.shape[2]
    heads_local = cols_local // HD
    block_len = patches + text_rows

    weight_t = doubling_gather(jnp.transpose(out_weight))

    img_full = gather_features(img_hidden)
    txt_rows = txt_hidden.reshape(requests * text_rows, -1)
    packed = jnp.concatenate([txt_rows, jnp.transpose(final_weight)], 0)
    packed = lax.all_gather(packed, "col", axis=0, tiled=False)
    slabs = packed.shape[0]
    txt_count = requests * text_rows
    txt_full = (
        jnp.moveaxis(packed[:, :txt_count], 0, -2)
        .reshape(txt_count, D)
        .reshape(requests, text_rows, D)
    )
    final_slabs = packed[:, txt_count:]
    normed = (layer_norm(img_full.astype(jnp.float32)) * (1.0 + img_mod[:, 1:2, :]) + img_mod[:, 0:1, :]).astype(
        jnp.bfloat16
    )
    flat_rows = normed.reshape(requests * patches, D)
    projected = jnp.einsum("td,cde->cte", flat_rows, qkv_weight, preferred_element_type=jnp.float32)
    queries = rms_heads(projected[0], qk_gains[0]).reshape(requests, patches, cols_local)
    img_keys = rms_heads(projected[1], qk_gains[1]).reshape(requests, patches, cols_local)
    img_values = projected[2].astype(jnp.bfloat16).reshape(requests, patches, cols_local)
    text_normed = (
        layer_norm(txt_full.astype(jnp.float32)) * (1.0 + txt_mod[:, 1:2, :]) + txt_mod[:, 0:1, :]
    ).astype(jnp.bfloat16)
    text_proj = jnp.einsum(
        "rtd,cde->crte", text_normed, txt_kv_weight, preferred_element_type=jnp.float32
    )
    text_keys = rms_heads(text_proj[0], qk_gains[2]).reshape(requests, text_rows, cols_local)
    text_values = text_proj[1].astype(jnp.bfloat16)
    key_rows = jnp.concatenate([img_keys, text_keys], 1)
    value_rows = jnp.concatenate([img_values, text_values], 1)

    def by_head(values, length):
        split = values.reshape(requests, length, heads_local, HD)
        return jnp.transpose(split, (0, 2, 1, 3)).reshape(requests * heads_local, length, HD)

    bundle = jnp.concatenate(
        [by_head(queries, patches), by_head(key_rows, block_len), by_head(value_rows, block_len)], 1
    )
    sources, bundle_rows = bundle.shape[0], bundle.shape[1]
    bundle = bundle.reshape(sources, bundle_rows // 2, 2 * HD)
    bundle = lax.all_to_all(bundle, ROW, 0, 0, tiled=True)
    bundle = bundle.reshape(sources, bundle_rows, HD)
    head_queries = bundle[:, :patches].reshape(sources * patches, HD)
    keys = bundle[:, patches : patches + block_len].reshape(sources * block_len, HD)
    values = bundle[:, patches + block_len :].reshape(sources * block_len, HD)

    request = lax.axis_index("rq")
    positions = jnp.arange(sources * block_len, dtype=jnp.int32)
    within = positions % block_len
    source_row = positions // block_len
    text_pos = source_row * text_rows + within - patches
    live_text = text_pos < lax.dynamic_index_in_dim(txt_len, request, keepdims=False)
    allowed = (within < patches) | live_text

    attended = attend_one(head_queries, keys, values, allowed).reshape(sources, patches, HD)
    attended = lax.all_to_all(attended, ROW, 0, 0, tiled=True)
    attended = jnp.transpose(
        attended.reshape(requests, heads_local, patches, HD), (0, 2, 1, 3)
    ).reshape(requests * patches, cols_local)

    partial_value = lax.dot_general(
        attended,
        weight_t,
        (((1,), (1,)), ((), ())),
        preferred_element_type=jnp.float32,
    )
    cols = lax.axis_size("col")
    col_index = lax.axis_index("col")
    shared_sum = halving_scatter(partial_value, cols, col_index)
    own_requests = requests // cols
    first = col_index * own_requests
    own_mods = lax.dynamic_slice_in_dim(img_mod, first, own_requests, 0)
    own_hidden = lax.dynamic_slice_in_dim(img_full, first, own_requests, 0).astype(jnp.float32)
    mixed = own_hidden + own_mods[:, 2:3, :] * shared_sum.reshape(own_requests, patches, D)
    modulated = (layer_norm(mixed) * (1.0 + own_mods[:, 4:5, :]) + own_mods[:, 3:4, :]).astype(
        jnp.bfloat16
    )
    velocity = jnp.einsum(
        "tcf,cof->to",
        modulated.reshape(own_requests * patches, slabs, D // slabs),
        final_slabs,
        preferred_element_type=jnp.float32,
    ).reshape(own_requests, patches, latent.shape[2])
    own_latent = lax.dynamic_slice_in_dim(latent, first, own_requests, 0)
    own_steps = lax.dynamic_slice_in_dim(step_idx, first, own_requests, 0)
    sigma_now = sigma_at(own_steps)[:, None, None]
    sigma_next = sigma_at(own_steps - 1)[:, None, None]
    advanced = own_latent + (sigma_next - sigma_now) * velocity
    denoised = own_latent - sigma_now * velocity
    both = lax.all_gather(jnp.stack([advanced, denoised]), "col", axis=1, tiled=True)
    advanced, denoised = both[0], both[1]
    return (advanced, denoised)


def solution(mesh):
    rows = mesh.shape["row"]
    cols = mesh.shape["col"]
    split = Mesh(mesh.devices.reshape(REQ, rows // REQ, cols), ("rq", "rm", "col"))
    in_specs = (
        P(None, ROW, "col"),
        P(None, ROW, "col"),
        P(None, ROW, None),
        P(),
        P(),
        P(None, None, "col"),
        P(None, None, "col"),
        P("col", ROW),
        P("col", None),
        P(),
        P(),
        P(),
    )
    out_specs = (P(None, ROW, None), P(None, ROW, None))
    return jax.shard_map(
        per_device, mesh=split, in_specs=in_specs, out_specs=out_specs, check_vma=False
    )
```

```python
import jax
import jax.numpy as jnp
from jax import lax
from jax.sharding import Mesh
from jax.sharding import PartitionSpec as P

D = 2432
HD = 64
STEPS = 28
REQ = 8

ROW = ("rq", "rm")

eps_norm = 1e-06
neg_fill = -1e30


def layer_norm(values):
    average = jnp.mean(values, -1, keepdims=True)
    centred = values - average
    variance = jnp.mean(centred * centred, -1, keepdims=True)
    return centred * lax.rsqrt(variance + eps_norm)


def rms_heads(values, scaling):
    reshaped = values.reshape(values.shape[:-1] + (values.shape[-1] // HD, HD))
    inverse = lax.rsqrt(jnp.mean(reshaped * reshaped, -1, keepdims=True) + eps_norm)
    return (reshaped * inverse * scaling).astype(jnp.bfloat16)


def sigma_at(indices):
    fraction = indices.astype(jnp.float32) / STEPS
    return 3.0 * fraction / (1.0 + 2.0 * fraction)


def doubling_gather(block, axis, order):
    size = lax.axis_size(axis)
    index = lax.axis_index(axis)
    bits = len(order)
    buffer = block[None]
    for bit in order:
        pairs = [(i, i ^ (1 << bit)) for i in range(size)]
        received = lax.ppermute(buffer, axis, pairs)
        upper = (index >> bit) % 2 == 1
        buffer = jnp.where(upper, jnp.stack([received, buffer]), jnp.stack([buffer, received]))
    done = list(reversed(order))
    buffer = buffer.reshape((2,) * bits + block.shape)
    perm = [done.index(bit) for bit in reversed(range(bits))]
    buffer = jnp.transpose(buffer, perm + list(range(bits, bits + block.ndim)))
    return buffer.reshape((size,) + block.shape)


COL_ORDER = [1, 0]


def gather_features(local):
    stacked = doubling_gather(local, "col", COL_ORDER)
    slabs = stacked.shape[0]
    moved = jnp.moveaxis(stacked, 0, -2)
    return moved.reshape(local.shape[:-1] + (slabs * local.shape[-1],))


def halving_scatter(partial, cols, col_index):
    rows = partial.shape[0] // cols
    chunks = partial.reshape((2, 2, rows) + partial.shape[1:])
    low = col_index % 2
    high = col_index // 2
    keep = lax.dynamic_index_in_dim(chunks, low, 1, keepdims=False)
    send = lax.dynamic_index_in_dim(chunks, 1 - low, 1, keepdims=False)
    pairs = [(i, i ^ 1) for i in range(cols)]
    halves = keep + lax.ppermute(send, "col", pairs)
    keep = lax.dynamic_index_in_dim(halves, high, 0, keepdims=False)
    send = lax.dynamic_index_in_dim(halves, 1 - high, 0, keepdims=False)
    pairs = [(i, i ^ 2) for i in range(cols)]
    return keep + lax.ppermute(send, "col", pairs)


def attend_one(queries, keys, values, allowed):
    scores = jnp.dot(queries, keys.T, preferred_element_type=jnp.float32) * HD ** (-0.5)
    scores = jnp.where(allowed[None, :], scores, neg_fill)
    top_score = jnp.max(scores, -1, keepdims=True)
    exp_scores = jnp.where(allowed[None, :], jnp.exp(scores - top_score), 0.0)
    row_total = jnp.sum(exp_scores, -1, keepdims=True)
    weighted = jnp.dot(exp_scores.astype(jnp.bfloat16), values, preferred_element_type=jnp.float32)
    return (weighted / row_total).astype(jnp.bfloat16)


def per_device(
    img_hidden,
    txt_hidden,
    latent,
    img_mod,
    txt_mod,
    qkv_weight,
    txt_kv_weight,
    out_weight,
    final_weight,
    qk_gains,
    txt_len,
    step_idx,
):
    requests = img_hidden.shape[0]
    patches = img_hidden.shape[1]
    text_rows = txt_hidden.shape[1]
    cols_local = qkv_weight.shape[2]
    heads_local = cols_local // HD
    block_len = patches + text_rows

    weight_t = lax.all_gather(jnp.transpose(out_weight), ROW, axis=0, tiled=True)

    img_full = gather_features(img_hidden)
    txt_rows = txt_hidden.reshape(requests * text_rows, -1)
    packed = jnp.concatenate([txt_rows, jnp.transpose(final_weight)], 0)
    packed = doubling_gather(packed, "col", COL_ORDER)
    slabs = packed.shape[0]
    txt_count = requests * text_rows
    txt_full = (
        jnp.moveaxis(packed[:, :txt_count], 0, -2)
        .reshape(txt_count, D)
        .reshape(requests, text_rows, D)
    )
    final_slabs = packed[:, txt_count:]
    normed = (layer_norm(img_full.astype(jnp.float32)) * (1.0 + img_mod[:, 1:2, :]) + img_mod[:, 0:1, :]).astype(
        jnp.bfloat16
    )
    flat_rows = normed.reshape(requests * patches, D)
    projected = jnp.einsum("td,cde->cte", flat_rows, qkv_weight, preferred_element_type=jnp.float32)
    queries = rms_heads(projected[0], qk_gains[0]).reshape(requests, patches, cols_local)
    img_keys = rms_heads(projected[1], qk_gains[1]).reshape(requests, patches, cols_local)
    img_values = projected[2].astype(jnp.bfloat16).reshape(requests, patches, cols_local)
    text_normed = (
        layer_norm(txt_full.astype(jnp.float32)) * (1.0 + txt_mod[:, 1:2, :]) + txt_mod[:, 0:1, :]
    ).astype(jnp.bfloat16)
    text_proj = jnp.einsum(
        "rtd,cde->crte", text_normed, txt_kv_weight, preferred_element_type=jnp.float32
    )
    text_keys = rms_heads(text_proj[0], qk_gains[2]).reshape(requests, text_rows, cols_local)
    text_values = text_proj[1].astype(jnp.bfloat16)
    key_rows = jnp.concatenate([img_keys, text_keys], 1)
    value_rows = jnp.concatenate([img_values, text_values], 1)

    def by_head(values, length):
        split = values.reshape(requests, length, heads_local, HD)
        return jnp.transpose(split, (0, 2, 1, 3)).reshape(requests * heads_local, length, HD)

    bundle = jnp.concatenate(
        [by_head(queries, patches), by_head(key_rows, block_len), by_head(value_rows, block_len)], 1
    )
    sources, bundle_rows = bundle.shape[0], bundle.shape[1]
    bundle = bundle.reshape(sources, bundle_rows // 2, 2 * HD)
    bundle = lax.all_to_all(bundle, ROW, 0, 0, tiled=True)
    bundle = bundle.reshape(sources, bundle_rows, HD)
    head_queries = bundle[:, :patches].reshape(sources * patches, HD)
    keys = bundle[:, patches : patches + block_len].reshape(sources * block_len, HD)
    values = bundle[:, patches + block_len :].reshape(sources * block_len, HD)

    request = lax.axis_index("rq")
    positions = jnp.arange(sources * block_len, dtype=jnp.int32)
    within = positions % block_len
    source_row = positions // block_len
    text_pos = source_row * text_rows + within - patches
    live_text = text_pos < lax.dynamic_index_in_dim(txt_len, request, keepdims=False)
    allowed = (within < patches) | live_text

    attended = attend_one(head_queries, keys, values, allowed).reshape(sources, patches, HD)
    attended = lax.all_to_all(attended, ROW, 0, 0, tiled=True)
    attended = jnp.transpose(
        attended.reshape(requests, heads_local, patches, HD), (0, 2, 1, 3)
    ).reshape(requests * patches, cols_local)

    partial_value = lax.dot_general(
        attended,
        weight_t,
        (((1,), (1,)), ((), ())),
        preferred_element_type=jnp.float32,
    )
    cols = lax.axis_size("col")
    col_index = lax.axis_index("col")
    shared_sum = halving_scatter(partial_value, cols, col_index)
    own_requests = requests // cols
    first = col_index * own_requests
    own_mods = lax.dynamic_slice_in_dim(img_mod, first, own_requests, 0)
    own_hidden = lax.dynamic_slice_in_dim(img_full, first, own_requests, 0).astype(jnp.float32)
    mixed = own_hidden + own_mods[:, 2:3, :] * shared_sum.reshape(own_requests, patches, D)
    modulated = (layer_norm(mixed) * (1.0 + own_mods[:, 4:5, :]) + own_mods[:, 3:4, :]).astype(
        jnp.bfloat16
    )
    velocity = jnp.einsum(
        "tcf,cof->to",
        modulated.reshape(own_requests * patches, slabs, D // slabs),
        final_slabs,
        preferred_element_type=jnp.float32,
    ).reshape(own_requests, patches, latent.shape[2])
    own_latent = lax.dynamic_slice_in_dim(latent, first, own_requests, 0)
    own_steps = lax.dynamic_slice_in_dim(step_idx, first, own_requests, 0)
    sigma_now = sigma_at(own_steps)[:, None, None]
    sigma_next = sigma_at(own_steps - 1)[:, None, None]
    advanced = own_latent + (sigma_next - sigma_now) * velocity
    denoised = own_latent - sigma_now * velocity
    both = doubling_gather(jnp.stack([advanced, denoised]), "col", COL_ORDER)
    both = jnp.moveaxis(both, 0, 1).reshape((2, requests) + both.shape[3:])
    advanced, denoised = both[0], both[1]
    return (advanced, denoised)


def solution(mesh):
    rows = mesh.shape["row"]
    cols = mesh.shape["col"]
    split = Mesh(mesh.devices.reshape(REQ, rows // REQ, cols), ("rq", "rm", "col"))
    in_specs = (
        P(None, ROW, "col"),
        P(None, ROW, "col"),
        P(None, ROW, None),
        P(),
        P(),
        P(None, None, "col"),
        P(None, None, "col"),
        P("col", ROW),
        P("col", None),
        P(),
        P(),
        P(),
    )
    out_specs = (P(None, ROW, None), P(None, ROW, None))
    return jax.shard_map(
        per_device, mesh=split, in_specs=in_specs, out_specs=out_specs, check_vma=False
    )
```

```python
import jax
import jax.numpy as jnp
from jax import lax
from jax.sharding import Mesh
from jax.sharding import PartitionSpec as P

D = 2432
HD = 64
STEPS = 28
REQ = 8

ROW = ("x", "zh", "y")

eps_norm = 1e-06
neg_fill = -1e30


def layer_norm(values):
    average = jnp.mean(values, -1, keepdims=True)
    centred = values - average
    variance = jnp.mean(centred * centred, -1, keepdims=True)
    return centred * lax.rsqrt(variance + eps_norm)


def rms_heads(values, scaling):
    reshaped = values.reshape(values.shape[:-1] + (values.shape[-1] // HD, HD))
    inverse = lax.rsqrt(jnp.mean(reshaped * reshaped, -1, keepdims=True) + eps_norm)
    return (reshaped * inverse * scaling).astype(jnp.bfloat16)


def sigma_at(indices):
    fraction = indices.astype(jnp.float32) / STEPS
    return 3.0 * fraction / (1.0 + 2.0 * fraction)


def doubling_gather(block, axis, order):
    size = lax.axis_size(axis)
    index = lax.axis_index(axis)
    bits = len(order)
    buffer = block[None]
    for bit in order:
        pairs = [(i, i ^ (1 << bit)) for i in range(size)]
        received = lax.ppermute(buffer, axis, pairs)
        upper = (index >> bit) % 2 == 1
        buffer = jnp.where(upper, jnp.stack([received, buffer]), jnp.stack([buffer, received]))
    done = list(reversed(order))
    buffer = buffer.reshape((2,) * bits + block.shape)
    perm = [done.index(bit) for bit in reversed(range(bits))]
    buffer = jnp.transpose(buffer, perm + list(range(bits, bits + block.ndim)))
    return buffer.reshape((size,) + block.shape)


COL_ORDER = [1, 0]


def gather_features(local):
    stacked = doubling_gather(local, "col", COL_ORDER)
    slabs = stacked.shape[0]
    moved = jnp.moveaxis(stacked, 0, -2)
    return moved.reshape(local.shape[:-1] + (slabs * local.shape[-1],))


def halving_scatter(partial, cols, col_index):
    rows = partial.shape[0] // cols
    chunks = partial.reshape((2, 2, rows) + partial.shape[1:])
    low = col_index % 2
    high = col_index // 2
    keep = lax.dynamic_index_in_dim(chunks, low, 1, keepdims=False)
    send = lax.dynamic_index_in_dim(chunks, 1 - low, 1, keepdims=False)
    pairs = [(i, i ^ 1) for i in range(cols)]
    halves = keep + lax.ppermute(send, "col", pairs)
    keep = lax.dynamic_index_in_dim(halves, high, 0, keepdims=False)
    send = lax.dynamic_index_in_dim(halves, 1 - high, 0, keepdims=False)
    pairs = [(i, i ^ 2) for i in range(cols)]
    return keep + lax.ppermute(send, "col", pairs)


def attend_one(queries, keys, values, allowed):
    scores = jnp.dot(queries, keys.T, preferred_element_type=jnp.float32) * HD ** (-0.5)
    scores = jnp.where(allowed[None, :], scores, neg_fill)
    top_score = jnp.max(scores, -1, keepdims=True)
    exp_scores = jnp.where(allowed[None, :], jnp.exp(scores - top_score), 0.0)
    row_total = jnp.sum(exp_scores, -1, keepdims=True)
    weighted = jnp.dot(exp_scores.astype(jnp.bfloat16), values, preferred_element_type=jnp.float32)
    return (weighted / row_total).astype(jnp.bfloat16)


def per_device(
    img_hidden,
    txt_hidden,
    latent,
    img_mod,
    txt_mod,
    qkv_weight,
    txt_kv_weight,
    out_weight,
    final_weight,
    qk_gains,
    txt_len,
    step_idx,
):
    requests = img_hidden.shape[0]
    patches = img_hidden.shape[1]
    text_rows = txt_hidden.shape[1]
    cols_local = qkv_weight.shape[2]
    heads_local = cols_local // HD
    block_len = patches + text_rows

    staged = lax.all_gather(jnp.transpose(out_weight), "zh", axis=0, tiled=False)
    staged = lax.all_gather(staged, "y", axis=0, tiled=False)
    staged = lax.all_gather(staged, "x", axis=0, tiled=False)
    weight_t = jnp.transpose(staged, (0, 2, 1, 3, 4)).reshape(-1, cols_local)

    img_full = gather_features(img_hidden)
    txt_rows = txt_hidden.reshape(requests * text_rows, -1)
    packed = jnp.concatenate([txt_rows, jnp.transpose(final_weight)], 0)
    packed = doubling_gather(packed, "col", COL_ORDER)
    slabs = packed.shape[0]
    txt_count = requests * text_rows
    txt_full = (
        jnp.moveaxis(packed[:, :txt_count], 0, -2)
        .reshape(txt_count, D)
        .reshape(requests, text_rows, D)
    )
    final_slabs = packed[:, txt_count:]
    normed = (layer_norm(img_full.astype(jnp.float32)) * (1.0 + img_mod[:, 1:2, :]) + img_mod[:, 0:1, :]).astype(
        jnp.bfloat16
    )
    flat_rows = normed.reshape(requests * patches, D)
    projected = jnp.einsum("td,cde->cte", flat_rows, qkv_weight, preferred_element_type=jnp.float32)
    queries = rms_heads(projected[0], qk_gains[0]).reshape(requests, patches, cols_local)
    img_keys = rms_heads(projected[1], qk_gains[1]).reshape(requests, patches, cols_local)
    img_values = projected[2].astype(jnp.bfloat16).reshape(requests, patches, cols_local)
    text_normed = (
        layer_norm(txt_full.astype(jnp.float32)) * (1.0 + txt_mod[:, 1:2, :]) + txt_mod[:, 0:1, :]
    ).astype(jnp.bfloat16)
    text_proj = jnp.einsum(
        "rtd,cde->crte", text_normed, txt_kv_weight, preferred_element_type=jnp.float32
    )
    text_keys = rms_heads(text_proj[0], qk_gains[2]).reshape(requests, text_rows, cols_local)
    text_values = text_proj[1].astype(jnp.bfloat16)
    key_rows = jnp.concatenate([img_keys, text_keys], 1)
    value_rows = jnp.concatenate([img_values, text_values], 1)

    def by_head(values, length):
        split = values.reshape(requests, length, heads_local, HD)
        return jnp.transpose(split, (0, 2, 1, 3)).reshape(requests * heads_local, length, HD)

    bundle = jnp.concatenate(
        [by_head(queries, patches), by_head(key_rows, block_len), by_head(value_rows, block_len)], 1
    )
    sources, bundle_rows = bundle.shape[0], bundle.shape[1]
    bundle = bundle.reshape(sources, bundle_rows // 2, 2 * HD)
    bundle = lax.all_to_all(bundle, ROW, 0, 0, tiled=True)
    bundle = bundle.reshape(sources, bundle_rows, HD)
    head_queries = bundle[:, :patches].reshape(sources * patches, HD)
    keys = bundle[:, patches : patches + block_len].reshape(sources * block_len, HD)
    values = bundle[:, patches + block_len :].reshape(sources * block_len, HD)

    request = lax.axis_index(ROW) // (sources // requests)
    positions = jnp.arange(sources * block_len, dtype=jnp.int32)
    within = positions % block_len
    source_row = positions // block_len
    text_pos = source_row * text_rows + within - patches
    live_text = text_pos < lax.dynamic_index_in_dim(txt_len, request, keepdims=False)
    allowed = (within < patches) | live_text

    attended = attend_one(head_queries, keys, values, allowed).reshape(sources, patches, HD)
    attended = lax.all_to_all(attended, ROW, 0, 0, tiled=True)
    attended = jnp.transpose(
        attended.reshape(requests, heads_local, patches, HD), (0, 2, 1, 3)
    ).reshape(requests * patches, cols_local)

    partial_value = lax.dot_general(
        attended,
        weight_t,
        (((1,), (1,)), ((), ())),
        preferred_element_type=jnp.float32,
    )
    cols = lax.axis_size("col")
    col_index = lax.axis_index("col")
    shared_sum = halving_scatter(partial_value, cols, col_index)
    own_requests = requests // cols
    first = col_index * own_requests
    own_mods = lax.dynamic_slice_in_dim(img_mod, first, own_requests, 0)
    own_hidden = lax.dynamic_slice_in_dim(img_full, first, own_requests, 0).astype(jnp.float32)
    mixed = own_hidden + own_mods[:, 2:3, :] * shared_sum.reshape(own_requests, patches, D)
    modulated = (layer_norm(mixed) * (1.0 + own_mods[:, 4:5, :]) + own_mods[:, 3:4, :]).astype(
        jnp.bfloat16
    )
    velocity = jnp.einsum(
        "tcf,cof->to",
        modulated.reshape(own_requests * patches, slabs, D // slabs),
        final_slabs,
        preferred_element_type=jnp.float32,
    ).reshape(own_requests, patches, latent.shape[2])
    own_latent = lax.dynamic_slice_in_dim(latent, first, own_requests, 0)
    own_steps = lax.dynamic_slice_in_dim(step_idx, first, own_requests, 0)
    sigma_now = sigma_at(own_steps)[:, None, None]
    sigma_next = sigma_at(own_steps - 1)[:, None, None]
    advanced = own_latent + (sigma_next - sigma_now) * velocity
    denoised = own_latent - sigma_now * velocity
    both = doubling_gather(jnp.stack([advanced, denoised]), "col", COL_ORDER)
    both = jnp.moveaxis(both, 0, 1).reshape((2, requests) + both.shape[3:])
    advanced, denoised = both[0], both[1]
    return (advanced, denoised)


def solution(mesh):
    rows = mesh.shape["row"]
    cols = mesh.shape["col"]
    side = round(rows ** (1 / 3))
    split = Mesh(mesh.devices.reshape(side, side, side, cols), ROW + ("col",))
    in_specs = (
        P(None, ROW, "col"),
        P(None, ROW, "col"),
        P(None, ROW, None),
        P(),
        P(),
        P(None, None, "col"),
        P(None, None, "col"),
        P("col", ROW),
        P("col", None),
        P(),
        P(),
        P(),
    )
    out_specs = (P(None, ROW, None), P(None, ROW, None))
    return jax.shard_map(
        per_device, mesh=split, in_specs=in_specs, out_specs=out_specs, check_vma=False
    )
```

```python
import jax
import jax.numpy as jnp
from jax import lax
from jax.sharding import Mesh
from jax.sharding import PartitionSpec as P

D = 2432
HD = 64
STEPS = 28
REQ = 8

ROW = ("rq", "rm")

eps_norm = 1e-06
neg_fill = -1e30


def layer_norm(values):
    average = jnp.mean(values, -1, keepdims=True)
    centred = values - average
    variance = jnp.mean(centred * centred, -1, keepdims=True)
    return centred * lax.rsqrt(variance + eps_norm)


def rms_heads(values, scaling):
    reshaped = values.reshape(values.shape[:-1] + (values.shape[-1] // HD, HD))
    inverse = lax.rsqrt(jnp.mean(reshaped * reshaped, -1, keepdims=True) + eps_norm)
    return (reshaped * inverse * scaling).astype(jnp.bfloat16)


def sigma_at(indices):
    fraction = indices.astype(jnp.float32) / STEPS
    return 3.0 * fraction / (1.0 + 2.0 * fraction)


def doubling_gather(block, axis, order):
    size = lax.axis_size(axis)
    index = lax.axis_index(axis)
    bits = len(order)
    buffer = block[None]
    for bit in order:
        pairs = [(i, i ^ (1 << bit)) for i in range(size)]
        received = lax.ppermute(buffer, axis, pairs)
        upper = (index >> bit) % 2 == 1
        buffer = jnp.where(upper, jnp.stack([received, buffer]), jnp.stack([buffer, received]))
    done = list(reversed(order))
    buffer = buffer.reshape((2,) * bits + block.shape)
    perm = [done.index(bit) for bit in reversed(range(bits))]
    buffer = jnp.transpose(buffer, perm + list(range(bits, bits + block.ndim)))
    return buffer.reshape((size,) + block.shape)


COL_ORDER = [1, 0]
ROW_ORDER = [3, 2, 5, 1, 4, 0]


def gather_features(local):
    stacked = doubling_gather(local, "col", COL_ORDER)
    slabs = stacked.shape[0]
    moved = jnp.moveaxis(stacked, 0, -2)
    return moved.reshape(local.shape[:-1] + (slabs * local.shape[-1],))


def halving_scatter(partial, cols, col_index):
    rows = partial.shape[0] // cols
    chunks = partial.reshape((2, 2, rows) + partial.shape[1:])
    low = col_index % 2
    high = col_index // 2
    keep = lax.dynamic_index_in_dim(chunks, low, 1, keepdims=False)
    send = lax.dynamic_index_in_dim(chunks, 1 - low, 1, keepdims=False)
    pairs = [(i, i ^ 1) for i in range(cols)]
    halves = keep + lax.ppermute(send, "col", pairs)
    keep = lax.dynamic_index_in_dim(halves, high, 0, keepdims=False)
    send = lax.dynamic_index_in_dim(halves, 1 - high, 0, keepdims=False)
    pairs = [(i, i ^ 2) for i in range(cols)]
    return keep + lax.ppermute(send, "col", pairs)


def attend_one(queries, keys, values, allowed):
    scores = jnp.dot(queries, keys.T, preferred_element_type=jnp.float32) * HD ** (-0.5)
    scores = jnp.where(allowed[None, :], scores, neg_fill)
    top_score = jnp.max(scores, -1, keepdims=True)
    exp_scores = jnp.where(allowed[None, :], jnp.exp(scores - top_score), 0.0)
    row_total = jnp.sum(exp_scores, -1, keepdims=True)
    weighted = jnp.dot(exp_scores.astype(jnp.bfloat16), values, preferred_element_type=jnp.float32)
    return (weighted / row_total).astype(jnp.bfloat16)


def per_device(
    img_hidden,
    txt_hidden,
    latent,
    img_mod,
    txt_mod,
    qkv_weight,
    txt_kv_weight,
    out_weight,
    final_weight,
    qk_gains,
    txt_len,
    step_idx,
):
    requests = img_hidden.shape[0]
    patches = img_hidden.shape[1]
    text_rows = txt_hidden.shape[1]
    cols_local = qkv_weight.shape[2]
    heads_local = cols_local // HD
    block_len = patches + text_rows


    img_full = gather_features(img_hidden)
    txt_rows = txt_hidden.reshape(requests * text_rows, -1)
    packed = jnp.concatenate([txt_rows, jnp.transpose(final_weight)], 0)
    packed = doubling_gather(packed, "col", COL_ORDER)
    slabs = packed.shape[0]
    txt_count = requests * text_rows
    txt_full = (
        jnp.moveaxis(packed[:, :txt_count], 0, -2)
        .reshape(txt_count, D)
        .reshape(requests, text_rows, D)
    )
    final_slabs = packed[:, txt_count:]
    normed = (layer_norm(img_full.astype(jnp.float32)) * (1.0 + img_mod[:, 1:2, :]) + img_mod[:, 0:1, :]).astype(
        jnp.bfloat16
    )
    flat_rows = normed.reshape(requests * patches, D)
    projected = jnp.einsum("td,cde->cte", flat_rows, qkv_weight, preferred_element_type=jnp.float32)
    queries = rms_heads(projected[0], qk_gains[0]).reshape(requests, patches, cols_local)
    img_keys = rms_heads(projected[1], qk_gains[1]).reshape(requests, patches, cols_local)
    img_values = projected[2].astype(jnp.bfloat16).reshape(requests, patches, cols_local)
    text_normed = (
        layer_norm(txt_full.astype(jnp.float32)) * (1.0 + txt_mod[:, 1:2, :]) + txt_mod[:, 0:1, :]
    ).astype(jnp.bfloat16)
    text_proj = jnp.einsum(
        "rtd,cde->crte", text_normed, txt_kv_weight, preferred_element_type=jnp.float32
    )
    text_keys = rms_heads(text_proj[0], qk_gains[2]).reshape(requests, text_rows, cols_local)
    text_values = text_proj[1].astype(jnp.bfloat16)
    key_rows = jnp.concatenate([img_keys, text_keys], 1)
    value_rows = jnp.concatenate([img_values, text_values], 1)

    def by_head(values, length):
        split = values.reshape(requests, length, heads_local, HD)
        return jnp.transpose(split, (0, 2, 1, 3)).reshape(requests * heads_local, length, HD)

    bundle = jnp.concatenate(
        [by_head(queries, patches), by_head(key_rows, block_len), by_head(value_rows, block_len)], 1
    )
    sources, bundle_rows = bundle.shape[0], bundle.shape[1]
    bundle = bundle.reshape(sources, bundle_rows // 2, 2 * HD)
    bundle, weight_block = lax.optimization_barrier((bundle, jnp.transpose(out_weight)))
    bundle = lax.all_to_all(bundle, ROW, 0, 0, tiled=True)
    weight_t = doubling_gather(weight_block, ROW, ROW_ORDER).reshape(-1, cols_local)
    bundle = bundle.reshape(sources, bundle_rows, HD)
    head_queries = bundle[:, :patches].reshape(sources * patches, HD)
    keys = bundle[:, patches : patches + block_len].reshape(sources * block_len, HD)
    values = bundle[:, patches + block_len :].reshape(sources * block_len, HD)

    request = lax.axis_index("rq")
    positions = jnp.arange(sources * block_len, dtype=jnp.int32)
    within = positions % block_len
    source_row = positions // block_len
    text_pos = source_row * text_rows + within - patches
    live_text = text_pos < lax.dynamic_index_in_dim(txt_len, request, keepdims=False)
    allowed = (within < patches) | live_text

    attended = attend_one(head_queries, keys, values, allowed).reshape(sources, patches, HD)
    attended = lax.all_to_all(attended, ROW, 0, 0, tiled=True)
    attended = jnp.transpose(
        attended.reshape(requests, heads_local, patches, HD), (0, 2, 1, 3)
    ).reshape(requests * patches, cols_local)

    partial_value = lax.dot_general(
        attended,
        weight_t,
        (((1,), (1,)), ((), ())),
        preferred_element_type=jnp.float32,
    )
    cols = lax.axis_size("col")
    col_index = lax.axis_index("col")
    shared_sum = halving_scatter(partial_value, cols, col_index)
    own_requests = requests // cols
    first = col_index * own_requests
    own_mods = lax.dynamic_slice_in_dim(img_mod, first, own_requests, 0)
    own_hidden = lax.dynamic_slice_in_dim(img_full, first, own_requests, 0).astype(jnp.float32)
    mixed = own_hidden + own_mods[:, 2:3, :] * shared_sum.reshape(own_requests, patches, D)
    modulated = (layer_norm(mixed) * (1.0 + own_mods[:, 4:5, :]) + own_mods[:, 3:4, :]).astype(
        jnp.bfloat16
    )
    velocity = jnp.einsum(
        "tcf,cof->to",
        modulated.reshape(own_requests * patches, slabs, D // slabs),
        final_slabs,
        preferred_element_type=jnp.float32,
    ).reshape(own_requests, patches, latent.shape[2])
    own_latent = lax.dynamic_slice_in_dim(latent, first, own_requests, 0)
    own_steps = lax.dynamic_slice_in_dim(step_idx, first, own_requests, 0)
    sigma_now = sigma_at(own_steps)[:, None, None]
    sigma_next = sigma_at(own_steps - 1)[:, None, None]
    advanced = own_latent + (sigma_next - sigma_now) * velocity
    denoised = own_latent - sigma_now * velocity
    both = doubling_gather(jnp.stack([advanced, denoised]), "col", COL_ORDER)
    both = jnp.moveaxis(both, 0, 1).reshape((2, requests) + both.shape[3:])
    advanced, denoised = both[0], both[1]
    return (advanced, denoised)


def solution(mesh):
    rows = mesh.shape["row"]
    cols = mesh.shape["col"]
    split = Mesh(mesh.devices.reshape(REQ, rows // REQ, cols), ("rq", "rm", "col"))
    in_specs = (
        P(None, ROW, "col"),
        P(None, ROW, "col"),
        P(None, ROW, None),
        P(),
        P(),
        P(None, None, "col"),
        P(None, None, "col"),
        P("col", ROW),
        P("col", None),
        P(),
        P(),
        P(),
    )
    out_specs = (P(None, ROW, None), P(None, ROW, None))
    return jax.shard_map(
        per_device, mesh=split, in_specs=in_specs, out_specs=out_specs, check_vma=False
    )
```

```python
import jax
import jax.numpy as jnp
from jax import lax
from jax.sharding import Mesh
from jax.sharding import PartitionSpec as P

D = 2432
HD = 64
STEPS = 28
REQ = 8

ROW = ("rq", "rm")

eps_norm = 1e-06
neg_fill = -1e30


def layer_norm(values):
    average = jnp.mean(values, -1, keepdims=True)
    centred = values - average
    variance = jnp.mean(centred * centred, -1, keepdims=True)
    return centred * lax.rsqrt(variance + eps_norm)


def rms_heads(values, scaling):
    reshaped = values.reshape(values.shape[:-1] + (values.shape[-1] // HD, HD))
    inverse = lax.rsqrt(jnp.mean(reshaped * reshaped, -1, keepdims=True) + eps_norm)
    return (reshaped * inverse * scaling).astype(jnp.bfloat16)


def sigma_at(indices):
    fraction = indices.astype(jnp.float32) / STEPS
    return 3.0 * fraction / (1.0 + 2.0 * fraction)


def doubling_gather(block, axis, order):
    size = lax.axis_size(axis)
    index = lax.axis_index(axis)
    bits = len(order)
    buffer = block[None]
    for bit in order:
        pairs = [(i, i ^ (1 << bit)) for i in range(size)]
        received = lax.ppermute(buffer, axis, pairs)
        upper = (index >> bit) % 2 == 1
        buffer = jnp.where(upper, jnp.stack([received, buffer]), jnp.stack([buffer, received]))
    done = list(reversed(order))
    buffer = buffer.reshape((2,) * bits + block.shape)
    perm = [done.index(bit) for bit in reversed(range(bits))]
    buffer = jnp.transpose(buffer, perm + list(range(bits, bits + block.ndim)))
    return buffer.reshape((size,) + block.shape)


COL_ORDER = [1, 0]


def gather_features(local):
    stacked = doubling_gather(local, "col", COL_ORDER)
    slabs = stacked.shape[0]
    moved = jnp.moveaxis(stacked, 0, -2)
    return moved.reshape(local.shape[:-1] + (slabs * local.shape[-1],))


def halving_scatter(partial, cols, col_index):
    rows = partial.shape[0] // cols
    chunks = partial.reshape((2, 2, rows) + partial.shape[1:])
    low = col_index % 2
    high = col_index // 2
    keep = lax.dynamic_index_in_dim(chunks, low, 1, keepdims=False)
    send = lax.dynamic_index_in_dim(chunks, 1 - low, 1, keepdims=False)
    pairs = [(i, i ^ 1) for i in range(cols)]
    halves = keep + lax.ppermute(send, "col", pairs)
    keep = lax.dynamic_index_in_dim(halves, high, 0, keepdims=False)
    send = lax.dynamic_index_in_dim(halves, 1 - high, 0, keepdims=False)
    pairs = [(i, i ^ 2) for i in range(cols)]
    return keep + lax.ppermute(send, "col", pairs)


def attend_one(queries, keys, values, allowed):
    scores = jnp.dot(queries, keys.T, preferred_element_type=jnp.float32) * HD ** (-0.5)
    scores = jnp.where(allowed[None, :], scores, neg_fill)
    top_score = jnp.max(scores, -1, keepdims=True)
    exp_scores = jnp.where(allowed[None, :], jnp.exp(scores - top_score), 0.0)
    row_total = jnp.sum(exp_scores, -1, keepdims=True)
    weighted = jnp.dot(exp_scores.astype(jnp.bfloat16), values, preferred_element_type=jnp.float32)
    return (weighted / row_total).astype(jnp.bfloat16)


def per_device(
    img_hidden,
    txt_hidden,
    latent,
    img_mod,
    txt_mod,
    qkv_weight,
    txt_kv_weight,
    out_weight,
    final_weight,
    qk_gains,
    txt_len,
    step_idx,
):
    requests = img_hidden.shape[0]
    patches = img_hidden.shape[1]
    text_rows = txt_hidden.shape[1]
    cols_local = qkv_weight.shape[2]
    heads_local = cols_local // HD
    block_len = patches + text_rows

    weight_t = lax.all_gather(jnp.transpose(out_weight), ROW, axis=0, tiled=True)

    img_full = gather_features(img_hidden)
    txt_rows = txt_hidden.reshape(requests * text_rows, -1)
    packed = jnp.concatenate([txt_rows, jnp.transpose(final_weight)], 0)
    packed = doubling_gather(packed, "col", COL_ORDER)
    slabs = packed.shape[0]
    txt_count = requests * text_rows
    txt_full = (
        jnp.moveaxis(packed[:, :txt_count], 0, -2)
        .reshape(txt_count, D)
        .reshape(requests, text_rows, D)
    )
    final_slabs = packed[:, txt_count:]
    normed = (layer_norm(img_full.astype(jnp.float32)) * (1.0 + img_mod[:, 1:2, :]) + img_mod[:, 0:1, :]).astype(
        jnp.bfloat16
    )
    flat_rows = normed.reshape(requests * patches, D)
    projected = jnp.einsum("td,cde->cte", flat_rows, qkv_weight, preferred_element_type=jnp.float32)
    queries = rms_heads(projected[0], qk_gains[0]).reshape(requests, patches, cols_local)
    img_keys = rms_heads(projected[1], qk_gains[1]).reshape(requests, patches, cols_local)
    img_values = projected[2].astype(jnp.bfloat16).reshape(requests, patches, cols_local)
    text_normed = (
        layer_norm(txt_full.astype(jnp.float32)) * (1.0 + txt_mod[:, 1:2, :]) + txt_mod[:, 0:1, :]
    ).astype(jnp.bfloat16)
    text_proj = jnp.einsum(
        "rtd,cde->crte", text_normed, txt_kv_weight, preferred_element_type=jnp.float32
    )
    text_keys = rms_heads(text_proj[0], qk_gains[2]).reshape(requests, text_rows, cols_local)
    text_values = text_proj[1].astype(jnp.bfloat16)
    key_rows = jnp.concatenate([img_keys, text_keys], 1)
    value_rows = jnp.concatenate([img_values, text_values], 1)

    def by_head(values, length):
        split = values.reshape(requests, length, heads_local, HD)
        return jnp.transpose(split, (0, 2, 1, 3)).reshape(requests * heads_local, length, HD)

    bundle = jnp.concatenate(
        [by_head(queries, patches), by_head(key_rows, block_len), by_head(value_rows, block_len)], 1
    )
    sources, bundle_rows = bundle.shape[0], bundle.shape[1]
    bundle = bundle.reshape(sources, bundle_rows // 2, 2 * HD)
    bundle = lax.all_to_all(bundle, ROW, 0, 0, tiled=True)
    bundle = bundle.reshape(sources, bundle_rows, HD)
    head_queries = bundle[:, :patches].reshape(sources * patches, HD)
    keys = bundle[:, patches : patches + block_len].reshape(sources * block_len, HD)
    values = bundle[:, patches + block_len :].reshape(sources * block_len, HD)

    request = lax.axis_index("rq")
    positions = jnp.arange(sources * block_len, dtype=jnp.int32)
    within = positions % block_len
    source_row = positions // block_len
    text_pos = source_row * text_rows + within - patches
    live_text = text_pos < lax.dynamic_index_in_dim(txt_len, request, keepdims=False)
    allowed = (within < patches) | live_text

    attended = attend_one(head_queries, keys, values, allowed).reshape(
        sources, patches // 2, 2 * HD
    )
    attended = lax.all_to_all(attended, ROW, 0, 0, tiled=True)
    attended = jnp.transpose(
        attended.reshape(requests, heads_local, patches, HD), (0, 2, 1, 3)
    ).reshape(requests * patches, cols_local)

    partial_value = lax.dot_general(
        attended,
        weight_t,
        (((1,), (1,)), ((), ())),
        preferred_element_type=jnp.float32,
    )
    cols = lax.axis_size("col")
    col_index = lax.axis_index("col")
    shared_sum = halving_scatter(partial_value, cols, col_index)
    own_requests = requests // cols
    first = col_index * own_requests
    own_mods = lax.dynamic_slice_in_dim(img_mod, first, own_requests, 0)
    own_hidden = lax.dynamic_slice_in_dim(img_full, first, own_requests, 0).astype(jnp.float32)
    mixed = own_hidden + own_mods[:, 2:3, :] * shared_sum.reshape(own_requests, patches, D)
    modulated = (layer_norm(mixed) * (1.0 + own_mods[:, 4:5, :]) + own_mods[:, 3:4, :]).astype(
        jnp.bfloat16
    )
    velocity = jnp.einsum(
        "tcf,cof->to",
        modulated.reshape(own_requests * patches, slabs, D // slabs),
        final_slabs,
        preferred_element_type=jnp.float32,
    ).reshape(own_requests, patches, latent.shape[2])
    own_latent = lax.dynamic_slice_in_dim(latent, first, own_requests, 0)
    own_steps = lax.dynamic_slice_in_dim(step_idx, first, own_requests, 0)
    sigma_now = sigma_at(own_steps)[:, None, None]
    sigma_next = sigma_at(own_steps - 1)[:, None, None]
    advanced = own_latent + (sigma_next - sigma_now) * velocity
    denoised = own_latent - sigma_now * velocity
    both = doubling_gather(jnp.stack([advanced, denoised]), "col", COL_ORDER)
    both = jnp.moveaxis(both, 0, 1).reshape((2, requests) + both.shape[3:])
    advanced, denoised = both[0], both[1]
    return (advanced, denoised)


def solution(mesh):
    rows = mesh.shape["row"]
    cols = mesh.shape["col"]
    split = Mesh(mesh.devices.reshape(REQ, rows // REQ, cols), ("rq", "rm", "col"))
    in_specs = (
        P(None, ROW, "col"),
        P(None, ROW, "col"),
        P(None, ROW, None),
        P(),
        P(),
        P(None, None, "col"),
        P(None, None, "col"),
        P("col", ROW),
        P("col", None),
        P(),
        P(),
        P(),
    )
    out_specs = (P(None, ROW, None), P(None, ROW, None))
    return jax.shard_map(
        per_device, mesh=split, in_specs=in_specs, out_specs=out_specs, check_vma=False
    )
```

```python
import jax
import jax.numpy as jnp
from jax import lax
from jax.sharding import Mesh
from jax.sharding import PartitionSpec as P

D = 2432
HD = 64
STEPS = 28
REQ = 8

ROW = ("rq", "rm")

eps_norm = 1e-06
neg_fill = -1e30


def layer_norm(values):
    average = jnp.mean(values, -1, keepdims=True)
    centred = values - average
    variance = jnp.mean(centred * centred, -1, keepdims=True)
    return centred * lax.rsqrt(variance + eps_norm)


def rms_heads(values, scaling):
    reshaped = values.reshape(values.shape[:-1] + (values.shape[-1] // HD, HD))
    inverse = lax.rsqrt(jnp.mean(reshaped * reshaped, -1, keepdims=True) + eps_norm)
    return (reshaped * inverse * scaling).astype(jnp.bfloat16)


def sigma_at(indices):
    fraction = indices.astype(jnp.float32) / STEPS
    return 3.0 * fraction / (1.0 + 2.0 * fraction)


def doubling_gather(block, axis, order):
    size = lax.axis_size(axis)
    index = lax.axis_index(axis)
    bits = len(order)
    buffer = block[None]
    for bit in order:
        pairs = [(i, i ^ (1 << bit)) for i in range(size)]
        received = lax.ppermute(buffer, axis, pairs)
        upper = (index >> bit) % 2 == 1
        buffer = jnp.where(upper, jnp.stack([received, buffer]), jnp.stack([buffer, received]))
    done = list(reversed(order))
    buffer = buffer.reshape((2,) * bits + block.shape)
    perm = [done.index(bit) for bit in reversed(range(bits))]
    buffer = jnp.transpose(buffer, perm + list(range(bits, bits + block.ndim)))
    return buffer.reshape((size,) + block.shape)


COL_ORDER = [1, 0]


def gather_features(local):
    stacked = doubling_gather(local, "col", COL_ORDER)
    slabs = stacked.shape[0]
    moved = jnp.moveaxis(stacked, 0, -2)
    return moved.reshape(local.shape[:-1] + (slabs * local.shape[-1],))


def halving_scatter(partial, cols, col_index):
    rows = partial.shape[0] // cols
    chunks = partial.reshape((2, 2, rows) + partial.shape[1:])
    low = col_index % 2
    high = col_index // 2
    keep = lax.dynamic_index_in_dim(chunks, low, 1, keepdims=False)
    send = lax.dynamic_index_in_dim(chunks, 1 - low, 1, keepdims=False)
    pairs = [(i, i ^ 1) for i in range(cols)]
    halves = keep + lax.ppermute(send, "col", pairs)
    keep = lax.dynamic_index_in_dim(halves, high, 0, keepdims=False)
    send = lax.dynamic_index_in_dim(halves, 1 - high, 0, keepdims=False)
    pairs = [(i, i ^ 2) for i in range(cols)]
    received = lax.ppermute(send.astype(jnp.bfloat16), "col", pairs)
    return keep + received.astype(jnp.float32)


def attend_one(queries, keys, values, allowed):
    scores = jnp.dot(queries, keys.T, preferred_element_type=jnp.float32) * HD ** (-0.5)
    scores = jnp.where(allowed[None, :], scores, neg_fill)
    top_score = jnp.max(scores, -1, keepdims=True)
    exp_scores = jnp.where(allowed[None, :], jnp.exp(scores - top_score), 0.0)
    row_total = jnp.sum(exp_scores, -1, keepdims=True)
    weighted = jnp.dot(exp_scores.astype(jnp.bfloat16), values, preferred_element_type=jnp.float32)
    return (weighted / row_total).astype(jnp.bfloat16)


def per_device(
    img_hidden,
    txt_hidden,
    latent,
    img_mod,
    txt_mod,
    qkv_weight,
    txt_kv_weight,
    out_weight,
    final_weight,
    qk_gains,
    txt_len,
    step_idx,
):
    requests = img_hidden.shape[0]
    patches = img_hidden.shape[1]
    text_rows = txt_hidden.shape[1]
    cols_local = qkv_weight.shape[2]
    heads_local = cols_local // HD
    block_len = patches + text_rows

    weight_t = lax.all_gather(jnp.transpose(out_weight), ROW, axis=0, tiled=True)

    img_full = gather_features(img_hidden)
    txt_rows = txt_hidden.reshape(requests * text_rows, -1)
    packed = jnp.concatenate([txt_rows, jnp.transpose(final_weight)], 0)
    packed = doubling_gather(packed, "col", COL_ORDER)
    slabs = packed.shape[0]
    txt_count = requests * text_rows
    txt_full = (
        jnp.moveaxis(packed[:, :txt_count], 0, -2)
        .reshape(txt_count, D)
        .reshape(requests, text_rows, D)
    )
    final_slabs = packed[:, txt_count:]
    normed = (layer_norm(img_full.astype(jnp.float32)) * (1.0 + img_mod[:, 1:2, :]) + img_mod[:, 0:1, :]).astype(
        jnp.bfloat16
    )
    flat_rows = normed.reshape(requests * patches, D)
    projected = jnp.einsum("td,cde->cte", flat_rows, qkv_weight, preferred_element_type=jnp.float32)
    queries = rms_heads(projected[0], qk_gains[0]).reshape(requests, patches, cols_local)
    img_keys = rms_heads(projected[1], qk_gains[1]).reshape(requests, patches, cols_local)
    img_values = projected[2].astype(jnp.bfloat16).reshape(requests, patches, cols_local)
    text_normed = (
        layer_norm(txt_full.astype(jnp.float32)) * (1.0 + txt_mod[:, 1:2, :]) + txt_mod[:, 0:1, :]
    ).astype(jnp.bfloat16)
    text_proj = jnp.einsum(
        "rtd,cde->crte", text_normed, txt_kv_weight, preferred_element_type=jnp.float32
    )
    text_keys = rms_heads(text_proj[0], qk_gains[2]).reshape(requests, text_rows, cols_local)
    text_values = text_proj[1].astype(jnp.bfloat16)
    key_rows = jnp.concatenate([img_keys, text_keys], 1)
    value_rows = jnp.concatenate([img_values, text_values], 1)

    def by_head(values, length):
        split = values.reshape(requests, length, heads_local, HD)
        return jnp.transpose(split, (0, 2, 1, 3)).reshape(requests * heads_local, length, HD)

    bundle = jnp.concatenate(
        [by_head(queries, patches), by_head(key_rows, block_len), by_head(value_rows, block_len)], 1
    )
    sources, bundle_rows = bundle.shape[0], bundle.shape[1]
    bundle = bundle.reshape(sources, bundle_rows // 2, 2 * HD)
    bundle = lax.all_to_all(bundle, ROW, 0, 0, tiled=True)
    bundle = bundle.reshape(sources, bundle_rows, HD)
    head_queries = bundle[:, :patches].reshape(sources * patches, HD)
    keys = bundle[:, patches : patches + block_len].reshape(sources * block_len, HD)
    values = bundle[:, patches + block_len :].reshape(sources * block_len, HD)

    request = lax.axis_index("rq")
    positions = jnp.arange(sources * block_len, dtype=jnp.int32)
    within = positions % block_len
    source_row = positions // block_len
    text_pos = source_row * text_rows + within - patches
    live_text = text_pos < lax.dynamic_index_in_dim(txt_len, request, keepdims=False)
    allowed = (within < patches) | live_text

    attended = attend_one(head_queries, keys, values, allowed).reshape(sources, patches, HD)
    attended = lax.all_to_all(attended, ROW, 0, 0, tiled=True)
    attended = jnp.transpose(
        attended.reshape(requests, heads_local, patches, HD), (0, 2, 1, 3)
    ).reshape(requests * patches, cols_local)

    partial_value = lax.dot_general(
        attended,
        weight_t,
        (((1,), (1,)), ((), ())),
        preferred_element_type=jnp.float32,
    )
    cols = lax.axis_size("col")
    col_index = lax.axis_index("col")
    shared_sum = halving_scatter(partial_value, cols, col_index)
    own_requests = requests // cols
    first = col_index * own_requests
    own_mods = lax.dynamic_slice_in_dim(img_mod, first, own_requests, 0)
    own_hidden = lax.dynamic_slice_in_dim(img_full, first, own_requests, 0).astype(jnp.float32)
    mixed = own_hidden + own_mods[:, 2:3, :] * shared_sum.reshape(own_requests, patches, D)
    modulated = (layer_norm(mixed) * (1.0 + own_mods[:, 4:5, :]) + own_mods[:, 3:4, :]).astype(
        jnp.bfloat16
    )
    velocity = jnp.einsum(
        "tcf,cof->to",
        modulated.reshape(own_requests * patches, slabs, D // slabs),
        final_slabs,
        preferred_element_type=jnp.float32,
    ).reshape(own_requests, patches, latent.shape[2])
    own_latent = lax.dynamic_slice_in_dim(latent, first, own_requests, 0)
    own_steps = lax.dynamic_slice_in_dim(step_idx, first, own_requests, 0)
    sigma_now = sigma_at(own_steps)[:, None, None]
    sigma_next = sigma_at(own_steps - 1)[:, None, None]
    advanced = own_latent + (sigma_next - sigma_now) * velocity
    denoised = own_latent - sigma_now * velocity
    both = doubling_gather(jnp.stack([advanced, denoised]), "col", COL_ORDER)
    both = jnp.moveaxis(both, 0, 1).reshape((2, requests) + both.shape[3:])
    advanced, denoised = both[0], both[1]
    return (advanced, denoised)


def solution(mesh):
    rows = mesh.shape["row"]
    cols = mesh.shape["col"]
    split = Mesh(mesh.devices.reshape(REQ, rows // REQ, cols), ("rq", "rm", "col"))
    in_specs = (
        P(None, ROW, "col"),
        P(None, ROW, "col"),
        P(None, ROW, None),
        P(),
        P(),
        P(None, None, "col"),
        P(None, None, "col"),
        P("col", ROW),
        P("col", None),
        P(),
        P(),
        P(),
    )
    out_specs = (P(None, ROW, None), P(None, ROW, None))
    return jax.shard_map(
        per_device, mesh=split, in_specs=in_specs, out_specs=out_specs, check_vma=False
    )
```

```python
import jax
import jax.numpy as jnp
from jax import lax
from jax.sharding import Mesh
from jax.sharding import PartitionSpec as P

D = 2432
HD = 64
STEPS = 28
REQ = 8

ROW = ("rq", "rm")

eps_norm = 1e-06
neg_fill = -1e30


def layer_norm(values):
    average = jnp.mean(values, -1, keepdims=True)
    centred = values - average
    variance = jnp.mean(centred * centred, -1, keepdims=True)
    return centred * lax.rsqrt(variance + eps_norm)


def rms_heads(values, scaling):
    reshaped = values.reshape(values.shape[:-1] + (values.shape[-1] // HD, HD))
    inverse = lax.rsqrt(jnp.mean(reshaped * reshaped, -1, keepdims=True) + eps_norm)
    return (reshaped * inverse * scaling).astype(jnp.bfloat16)


def sigma_at(indices):
    fraction = indices.astype(jnp.float32) / STEPS
    return 3.0 * fraction / (1.0 + 2.0 * fraction)


def doubling_gather(block, axis, order):
    size = lax.axis_size(axis)
    index = lax.axis_index(axis)
    bits = len(order)
    buffer = block[None]
    for bit in order:
        pairs = [(i, i ^ (1 << bit)) for i in range(size)]
        received = lax.ppermute(buffer, axis, pairs)
        upper = (index >> bit) % 2 == 1
        buffer = jnp.where(upper, jnp.stack([received, buffer]), jnp.stack([buffer, received]))
    done = list(reversed(order))
    buffer = buffer.reshape((2,) * bits + block.shape)
    perm = [done.index(bit) for bit in reversed(range(bits))]
    buffer = jnp.transpose(buffer, perm + list(range(bits, bits + block.ndim)))
    return buffer.reshape((size,) + block.shape)


COL_ORDER = [1, 0]


def gather_features(local):
    stacked = doubling_gather(local, "col", COL_ORDER)
    slabs = stacked.shape[0]
    moved = jnp.moveaxis(stacked, 0, -2)
    return moved.reshape(local.shape[:-1] + (slabs * local.shape[-1],))


def halving_scatter(partial, cols, col_index):
    rows = partial.shape[0] // cols
    chunks = partial.reshape((2, 2, rows) + partial.shape[1:])
    low = col_index % 2
    high = col_index // 2
    keep = lax.dynamic_index_in_dim(chunks, low, 1, keepdims=False)
    send = lax.dynamic_index_in_dim(chunks, 1 - low, 1, keepdims=False)
    pairs = [(i, i ^ 1) for i in range(cols)]
    halves = keep + lax.ppermute(send, "col", pairs)
    keep = lax.dynamic_index_in_dim(halves, high, 0, keepdims=False)
    send = lax.dynamic_index_in_dim(halves, 1 - high, 0, keepdims=False)
    pairs = [(i, i ^ 2) for i in range(cols)]
    received = lax.ppermute(send.astype(jnp.bfloat16), "col", pairs)
    return keep + received.astype(jnp.float32)


def attend_one(queries, keys, values, allowed):
    scores = jnp.dot(queries, keys.T, preferred_element_type=jnp.float32) * HD ** (-0.5)
    scores = jnp.where(allowed[None, :], scores, neg_fill)
    top_score = jnp.max(scores, -1, keepdims=True)
    exp_scores = jnp.where(allowed[None, :], jnp.exp(scores - top_score), 0.0)
    row_total = jnp.sum(exp_scores, -1, keepdims=True)
    weighted = jnp.dot(exp_scores.astype(jnp.bfloat16), values, preferred_element_type=jnp.float32)
    return (weighted / row_total).astype(jnp.bfloat16)


def per_device(
    img_hidden,
    txt_hidden,
    latent,
    img_mod,
    txt_mod,
    qkv_weight,
    txt_kv_weight,
    out_weight,
    final_weight,
    qk_gains,
    txt_len,
    step_idx,
):
    requests = img_hidden.shape[0]
    patches = img_hidden.shape[1]
    text_rows = txt_hidden.shape[1]
    cols_local = qkv_weight.shape[2]
    heads_local = cols_local // HD
    block_len = patches + text_rows

    weight_t = lax.all_gather(jnp.transpose(out_weight), ROW, axis=0, tiled=True)

    img_full = gather_features(img_hidden)
    txt_rows = txt_hidden.reshape(requests * text_rows, -1)
    packed = jnp.concatenate([txt_rows, jnp.transpose(final_weight)], 0)
    packed = doubling_gather(packed, "col", COL_ORDER)
    slabs = packed.shape[0]
    txt_count = requests * text_rows
    txt_full = (
        jnp.moveaxis(packed[:, :txt_count], 0, -2)
        .reshape(txt_count, D)
        .reshape(requests, text_rows, D)
    )
    final_slabs = packed[:, txt_count:]
    normed = (layer_norm(img_full.astype(jnp.float32)) * (1.0 + img_mod[:, 1:2, :]) + img_mod[:, 0:1, :]).astype(
        jnp.bfloat16
    )
    flat_rows = normed.reshape(requests * patches, D)
    projected = jnp.einsum("td,cde->cte", flat_rows, qkv_weight, preferred_element_type=jnp.float32)
    queries = rms_heads(projected[0], qk_gains[0]).reshape(requests, patches, cols_local)
    img_keys = rms_heads(projected[1], qk_gains[1]).reshape(requests, patches, cols_local)
    img_values = projected[2].astype(jnp.bfloat16).reshape(requests, patches, cols_local)
    text_normed = (
        layer_norm(txt_full.astype(jnp.float32)) * (1.0 + txt_mod[:, 1:2, :]) + txt_mod[:, 0:1, :]
    ).astype(jnp.bfloat16)
    text_proj = jnp.einsum(
        "rtd,cde->crte", text_normed, txt_kv_weight, preferred_element_type=jnp.float32
    )
    text_keys = rms_heads(text_proj[0], qk_gains[2]).reshape(requests, text_rows, cols_local)
    text_values = text_proj[1].astype(jnp.bfloat16)
    key_rows = jnp.concatenate([img_keys, text_keys], 1)
    value_rows = jnp.concatenate([img_values, text_values], 1)

    def by_head(values, length):
        split = values.reshape(requests, length, heads_local, HD)
        return jnp.transpose(split, (0, 2, 1, 3)).reshape(requests * heads_local, length, HD)

    bundle = jnp.concatenate(
        [by_head(queries, patches), by_head(key_rows, block_len), by_head(value_rows, block_len)], 1
    )
    sources, bundle_rows = bundle.shape[0], bundle.shape[1]
    bundle = bundle.reshape(sources, bundle_rows // 2, 2 * HD)
    bundle = lax.all_to_all(bundle, ROW, 0, 0, tiled=True)
    bundle = bundle.reshape(sources, bundle_rows, HD)
    head_queries = bundle[:, :patches].reshape(sources * patches, HD)
    keys = bundle[:, patches : patches + block_len].reshape(sources * block_len, HD)
    values = bundle[:, patches + block_len :].reshape(sources * block_len, HD)

    request = lax.axis_index("rq")
    positions = jnp.arange(sources * block_len, dtype=jnp.int32)
    within = positions % block_len
    source_row = positions // block_len
    text_pos = source_row * text_rows + within - patches
    live_text = text_pos < lax.dynamic_index_in_dim(txt_len, request, keepdims=False)
    allowed = (within < patches) | live_text

    attended = attend_one(head_queries, keys, values, allowed).reshape(sources, patches, HD)
    attended = lax.all_to_all(attended, ROW, 0, 0, tiled=True)
    partial_value = jnp.einsum(
        "rhtd,nhd->rtn",
        attended.reshape(requests, heads_local, patches, HD),
        weight_t.reshape(-1, heads_local, HD),
        preferred_element_type=jnp.float32,
    ).reshape(requests * patches, -1)
    cols = lax.axis_size("col")
    col_index = lax.axis_index("col")
    shared_sum = halving_scatter(partial_value, cols, col_index)
    own_requests = requests // cols
    first = col_index * own_requests
    own_mods = lax.dynamic_slice_in_dim(img_mod, first, own_requests, 0)
    own_hidden = lax.dynamic_slice_in_dim(img_full, first, own_requests, 0).astype(jnp.float32)
    mixed = own_hidden + own_mods[:, 2:3, :] * shared_sum.reshape(own_requests, patches, D)
    modulated = (layer_norm(mixed) * (1.0 + own_mods[:, 4:5, :]) + own_mods[:, 3:4, :]).astype(
        jnp.bfloat16
    )
    velocity = jnp.einsum(
        "tcf,cof->to",
        modulated.reshape(own_requests * patches, slabs, D // slabs),
        final_slabs,
        preferred_element_type=jnp.float32,
    ).reshape(own_requests, patches, latent.shape[2])
    own_latent = lax.dynamic_slice_in_dim(latent, first, own_requests, 0)
    own_steps = lax.dynamic_slice_in_dim(step_idx, first, own_requests, 0)
    sigma_now = sigma_at(own_steps)[:, None, None]
    sigma_next = sigma_at(own_steps - 1)[:, None, None]
    advanced = own_latent + (sigma_next - sigma_now) * velocity
    denoised = own_latent - sigma_now * velocity
    both = doubling_gather(jnp.stack([advanced, denoised]), "col", COL_ORDER)
    both = jnp.moveaxis(both, 0, 1).reshape((2, requests) + both.shape[3:])
    advanced, denoised = both[0], both[1]
    return (advanced, denoised)


def solution(mesh):
    rows = mesh.shape["row"]
    cols = mesh.shape["col"]
    split = Mesh(mesh.devices.reshape(REQ, rows // REQ, cols), ("rq", "rm", "col"))
    in_specs = (
        P(None, ROW, "col"),
        P(None, ROW, "col"),
        P(None, ROW, None),
        P(),
        P(),
        P(None, None, "col"),
        P(None, None, "col"),
        P("col", ROW),
        P("col", None),
        P(),
        P(),
        P(),
    )
    out_specs = (P(None, ROW, None), P(None, ROW, None))
    return jax.shard_map(
        per_device, mesh=split, in_specs=in_specs, out_specs=out_specs, check_vma=False
    )
```

```python
import jax
import jax.numpy as jnp
from jax import lax
from jax.sharding import Mesh
from jax.sharding import PartitionSpec as P

D = 2432
HD = 64
STEPS = 28
REQ = 8

ROW = ("rq", "rm")

eps_norm = 1e-06
neg_fill = -1e30


def layer_norm(values):
    average = jnp.mean(values, -1, keepdims=True)
    centred = values - average
    variance = jnp.mean(centred * centred, -1, keepdims=True)
    return centred * lax.rsqrt(variance + eps_norm)


def rms_heads(values, scaling):
    reshaped = values.reshape(values.shape[:-1] + (values.shape[-1] // HD, HD))
    inverse = lax.rsqrt(jnp.mean(reshaped * reshaped, -1, keepdims=True) + eps_norm)
    return (reshaped * inverse * scaling).astype(jnp.bfloat16)


def sigma_at(indices):
    fraction = indices.astype(jnp.float32) / STEPS
    return 3.0 * fraction / (1.0 + 2.0 * fraction)


def doubling_gather(block, axis, order):
    size = lax.axis_size(axis)
    index = lax.axis_index(axis)
    bits = len(order)
    buffer = block[None]
    for bit in order:
        pairs = [(i, i ^ (1 << bit)) for i in range(size)]
        received = lax.ppermute(buffer, axis, pairs)
        upper = (index >> bit) % 2 == 1
        buffer = jnp.where(upper, jnp.stack([received, buffer]), jnp.stack([buffer, received]))
    done = list(reversed(order))
    buffer = buffer.reshape((2,) * bits + block.shape)
    perm = [done.index(bit) for bit in reversed(range(bits))]
    buffer = jnp.transpose(buffer, perm + list(range(bits, bits + block.ndim)))
    return buffer.reshape((size,) + block.shape)


COL_ORDER = [1, 0]


def gather_features(local):
    stacked = doubling_gather(local, "col", COL_ORDER)
    slabs = stacked.shape[0]
    moved = jnp.moveaxis(stacked, 0, -2)
    return moved.reshape(local.shape[:-1] + (slabs * local.shape[-1],))


def halving_scatter(partial, cols, col_index):
    rows = partial.shape[0] // cols
    chunks = partial.reshape((2, 2, rows) + partial.shape[1:])
    low = col_index % 2
    high = col_index // 2
    keep = lax.dynamic_index_in_dim(chunks, low, 1, keepdims=False)
    send = lax.dynamic_index_in_dim(chunks, 1 - low, 1, keepdims=False)
    pairs = [(i, i ^ 1) for i in range(cols)]
    halves = keep + lax.ppermute(send, "col", pairs)
    keep = lax.dynamic_index_in_dim(halves, high, 0, keepdims=False)
    send = lax.dynamic_index_in_dim(halves, 1 - high, 0, keepdims=False)
    pairs = [(i, i ^ 2) for i in range(cols)]
    received = lax.ppermute(send.astype(jnp.bfloat16), "col", pairs)
    return keep + received.astype(jnp.float32)


def attend_one(queries, keys, values, allowed):
    scores = jnp.dot(queries, keys.T, preferred_element_type=jnp.float32) * HD ** (-0.5)
    scores = jnp.where(allowed[None, :], scores, neg_fill)
    top_score = jnp.max(scores, -1, keepdims=True)
    exp_scores = jnp.where(allowed[None, :], jnp.exp(scores - top_score), 0.0)
    row_total = jnp.sum(exp_scores, -1, keepdims=True)
    weighted = jnp.dot(exp_scores.astype(jnp.bfloat16), values, preferred_element_type=jnp.float32)
    return (weighted / row_total).astype(jnp.bfloat16)


def per_device(
    img_hidden,
    txt_hidden,
    latent,
    img_mod,
    txt_mod,
    qkv_weight,
    txt_kv_weight,
    out_weight,
    final_weight,
    qk_gains,
    txt_len,
    step_idx,
):
    requests = img_hidden.shape[0]
    patches = img_hidden.shape[1]
    text_rows = txt_hidden.shape[1]
    cols_local = qkv_weight.shape[2]
    heads_local = cols_local // HD
    block_len = patches + text_rows

    weight_t = lax.all_gather(jnp.transpose(out_weight), ROW, axis=0, tiled=True)

    img_full = lax.optimization_barrier(gather_features(img_hidden))
    txt_rows = txt_hidden.reshape(requests * text_rows, -1)
    packed = jnp.concatenate([txt_rows, jnp.transpose(final_weight)], 0)
    packed = doubling_gather(packed, "col", COL_ORDER)
    slabs = packed.shape[0]
    txt_count = requests * text_rows
    txt_full = (
        jnp.moveaxis(packed[:, :txt_count], 0, -2)
        .reshape(txt_count, D)
        .reshape(requests, text_rows, D)
    )
    final_slabs = packed[:, txt_count:]
    normed = (layer_norm(img_full.astype(jnp.float32)) * (1.0 + img_mod[:, 1:2, :]) + img_mod[:, 0:1, :]).astype(
        jnp.bfloat16
    )
    flat_rows = normed.reshape(requests * patches, D)
    projected = jnp.einsum("td,cde->cte", flat_rows, qkv_weight, preferred_element_type=jnp.float32)
    queries = rms_heads(projected[0], qk_gains[0]).reshape(requests, patches, cols_local)
    img_keys = rms_heads(projected[1], qk_gains[1]).reshape(requests, patches, cols_local)
    img_values = projected[2].astype(jnp.bfloat16).reshape(requests, patches, cols_local)
    text_normed = (
        layer_norm(txt_full.astype(jnp.float32)) * (1.0 + txt_mod[:, 1:2, :]) + txt_mod[:, 0:1, :]
    ).astype(jnp.bfloat16)
    text_proj = jnp.einsum(
        "rtd,cde->crte", text_normed, txt_kv_weight, preferred_element_type=jnp.float32
    )
    text_keys = rms_heads(text_proj[0], qk_gains[2]).reshape(requests, text_rows, cols_local)
    text_values = text_proj[1].astype(jnp.bfloat16)
    key_rows = jnp.concatenate([img_keys, text_keys], 1)
    value_rows = jnp.concatenate([img_values, text_values], 1)

    def by_head(values, length):
        split = values.reshape(requests, length, heads_local, HD)
        return jnp.transpose(split, (0, 2, 1, 3)).reshape(requests * heads_local, length, HD)

    bundle = jnp.concatenate(
        [by_head(queries, patches), by_head(key_rows, block_len), by_head(value_rows, block_len)], 1
    )
    sources, bundle_rows = bundle.shape[0], bundle.shape[1]
    bundle = bundle.reshape(sources, bundle_rows // 2, 2 * HD)
    bundle = lax.all_to_all(bundle, ROW, 0, 0, tiled=True)
    bundle = bundle.reshape(sources, bundle_rows, HD)
    head_queries = bundle[:, :patches].reshape(sources * patches, HD)
    keys = bundle[:, patches : patches + block_len].reshape(sources * block_len, HD)
    values = bundle[:, patches + block_len :].reshape(sources * block_len, HD)

    request = lax.axis_index("rq")
    positions = jnp.arange(sources * block_len, dtype=jnp.int32)
    within = positions % block_len
    source_row = positions // block_len
    text_pos = source_row * text_rows + within - patches
    live_text = text_pos < lax.dynamic_index_in_dim(txt_len, request, keepdims=False)
    allowed = (within < patches) | live_text

    attended = attend_one(head_queries, keys, values, allowed).reshape(sources, patches, HD)
    attended = lax.all_to_all(attended, ROW, 0, 0, tiled=True)
    attended = jnp.transpose(
        attended.reshape(requests, heads_local, patches, HD), (0, 2, 1, 3)
    ).reshape(requests * patches, cols_local)

    partial_value = lax.dot_general(
        attended,
        weight_t,
        (((1,), (1,)), ((), ())),
        preferred_element_type=jnp.float32,
    )
    cols = lax.axis_size("col")
    col_index = lax.axis_index("col")
    shared_sum = halving_scatter(partial_value, cols, col_index)
    own_requests = requests // cols
    first = col_index * own_requests
    own_mods = lax.dynamic_slice_in_dim(img_mod, first, own_requests, 0)
    own_hidden = lax.dynamic_slice_in_dim(img_full, first, own_requests, 0).astype(jnp.float32)
    mixed = own_hidden + own_mods[:, 2:3, :] * shared_sum.reshape(own_requests, patches, D)
    modulated = (layer_norm(mixed) * (1.0 + own_mods[:, 4:5, :]) + own_mods[:, 3:4, :]).astype(
        jnp.bfloat16
    )
    velocity = jnp.einsum(
        "tcf,cof->to",
        modulated.reshape(own_requests * patches, slabs, D // slabs),
        final_slabs,
        preferred_element_type=jnp.float32,
    ).reshape(own_requests, patches, latent.shape[2])
    own_latent = lax.dynamic_slice_in_dim(latent, first, own_requests, 0)
    own_steps = lax.dynamic_slice_in_dim(step_idx, first, own_requests, 0)
    sigma_now = sigma_at(own_steps)[:, None, None]
    sigma_next = sigma_at(own_steps - 1)[:, None, None]
    advanced = own_latent + (sigma_next - sigma_now) * velocity
    denoised = own_latent - sigma_now * velocity
    both = doubling_gather(jnp.stack([advanced, denoised]), "col", COL_ORDER)
    both = jnp.moveaxis(both, 0, 1).reshape((2, requests) + both.shape[3:])
    advanced, denoised = both[0], both[1]
    return (advanced, denoised)


def solution(mesh):
    rows = mesh.shape["row"]
    cols = mesh.shape["col"]
    split = Mesh(mesh.devices.reshape(REQ, rows // REQ, cols), ("rq", "rm", "col"))
    in_specs = (
        P(None, ROW, "col"),
        P(None, ROW, "col"),
        P(None, ROW, None),
        P(),
        P(),
        P(None, None, "col"),
        P(None, None, "col"),
        P("col", ROW),
        P("col", None),
        P(),
        P(),
        P(),
    )
    out_specs = (P(None, ROW, None), P(None, ROW, None))
    return jax.shard_map(
        per_device, mesh=split, in_specs=in_specs, out_specs=out_specs, check_vma=False
    )
```

```python
import jax
import jax.numpy as jnp
from jax import lax
from jax.sharding import Mesh
from jax.sharding import PartitionSpec as P

D = 2432
HD = 64
STEPS = 28
REQ = 8

ROW = ("rq", "rm")

eps_norm = 1e-06
neg_fill = -1e30


def layer_norm(values):
    average = jnp.mean(values, -1, keepdims=True)
    centred = values - average
    variance = jnp.mean(centred * centred, -1, keepdims=True)
    return centred * lax.rsqrt(variance + eps_norm)


def rms_heads(values, scaling):
    reshaped = values.reshape(values.shape[:-1] + (values.shape[-1] // HD, HD))
    inverse = lax.rsqrt(jnp.mean(reshaped * reshaped, -1, keepdims=True) + eps_norm)
    return (reshaped * inverse * scaling).astype(jnp.bfloat16)


def sigma_at(indices):
    fraction = indices.astype(jnp.float32) / STEPS
    return 3.0 * fraction / (1.0 + 2.0 * fraction)


def doubling_gather(block, axis, order):
    size = lax.axis_size(axis)
    index = lax.axis_index(axis)
    bits = len(order)
    buffer = block[None]
    for bit in order:
        pairs = [(i, i ^ (1 << bit)) for i in range(size)]
        received = lax.ppermute(buffer, axis, pairs)
        upper = (index >> bit) % 2 == 1
        buffer = jnp.where(upper, jnp.stack([received, buffer]), jnp.stack([buffer, received]))
    done = list(reversed(order))
    buffer = buffer.reshape((2,) * bits + block.shape)
    perm = [done.index(bit) for bit in reversed(range(bits))]
    buffer = jnp.transpose(buffer, perm + list(range(bits, bits + block.ndim)))
    return buffer.reshape((size,) + block.shape)


COL_ORDER = [1, 0]


def gather_features(local):
    stacked = doubling_gather(local, "col", COL_ORDER)
    slabs = stacked.shape[0]
    moved = jnp.moveaxis(stacked, 0, -2)
    return moved.reshape(local.shape[:-1] + (slabs * local.shape[-1],))


def halving_scatter(partial, cols, col_index):
    rows = partial.shape[0] // cols
    chunks = partial.reshape((2, 2, rows) + partial.shape[1:])
    low = col_index % 2
    high = col_index // 2
    keep = lax.dynamic_index_in_dim(chunks, low, 1, keepdims=False)
    send = lax.dynamic_index_in_dim(chunks, 1 - low, 1, keepdims=False)
    pairs = [(i, i ^ 1) for i in range(cols)]
    halves = keep + lax.ppermute(send.astype(jnp.bfloat16), "col", pairs).astype(jnp.float32)
    keep = lax.dynamic_index_in_dim(halves, high, 0, keepdims=False)
    send = lax.dynamic_index_in_dim(halves, 1 - high, 0, keepdims=False)
    pairs = [(i, i ^ 2) for i in range(cols)]
    received = lax.ppermute(send.astype(jnp.bfloat16), "col", pairs)
    return keep + received.astype(jnp.float32)


def attend_one(queries, keys, values, allowed):
    scores = jnp.dot(queries, keys.T, preferred_element_type=jnp.float32) * HD ** (-0.5)
    scores = jnp.where(allowed[None, :], scores, neg_fill)
    top_score = jnp.max(scores, -1, keepdims=True)
    exp_scores = jnp.where(allowed[None, :], jnp.exp(scores - top_score), 0.0)
    row_total = jnp.sum(exp_scores, -1, keepdims=True)
    weighted = jnp.dot(exp_scores.astype(jnp.bfloat16), values, preferred_element_type=jnp.float32)
    return (weighted / row_total).astype(jnp.bfloat16)


def per_device(
    img_hidden,
    txt_hidden,
    latent,
    img_mod,
    txt_mod,
    qkv_weight,
    txt_kv_weight,
    out_weight,
    final_weight,
    qk_gains,
    txt_len,
    step_idx,
):
    requests = img_hidden.shape[0]
    patches = img_hidden.shape[1]
    text_rows = txt_hidden.shape[1]
    cols_local = qkv_weight.shape[2]
    heads_local = cols_local // HD
    block_len = patches + text_rows

    weight_t = lax.all_gather(jnp.transpose(out_weight), ROW, axis=0, tiled=True)

    img_full = lax.optimization_barrier(gather_features(img_hidden))
    txt_rows = txt_hidden.reshape(requests * text_rows, -1)
    packed = jnp.concatenate([txt_rows, jnp.transpose(final_weight)], 0)
    packed = doubling_gather(packed, "col", COL_ORDER)
    slabs = packed.shape[0]
    txt_count = requests * text_rows
    txt_full = (
        jnp.moveaxis(packed[:, :txt_count], 0, -2)
        .reshape(txt_count, D)
        .reshape(requests, text_rows, D)
    )
    final_slabs = packed[:, txt_count:]
    normed = (layer_norm(img_full.astype(jnp.float32)) * (1.0 + img_mod[:, 1:2, :]) + img_mod[:, 0:1, :]).astype(
        jnp.bfloat16
    )
    flat_rows = normed.reshape(requests * patches, D)
    projected = jnp.einsum("td,cde->cte", flat_rows, qkv_weight, preferred_element_type=jnp.float32)
    queries = rms_heads(projected[0], qk_gains[0]).reshape(requests, patches, cols_local)
    img_keys = rms_heads(projected[1], qk_gains[1]).reshape(requests, patches, cols_local)
    img_values = projected[2].astype(jnp.bfloat16).reshape(requests, patches, cols_local)
    text_normed = (
        layer_norm(txt_full.astype(jnp.float32)) * (1.0 + txt_mod[:, 1:2, :]) + txt_mod[:, 0:1, :]
    ).astype(jnp.bfloat16)
    text_proj = jnp.einsum(
        "rtd,cde->crte", text_normed, txt_kv_weight, preferred_element_type=jnp.float32
    )
    text_keys = rms_heads(text_proj[0], qk_gains[2]).reshape(requests, text_rows, cols_local)
    text_values = text_proj[1].astype(jnp.bfloat16)
    key_rows = jnp.concatenate([img_keys, text_keys], 1)
    value_rows = jnp.concatenate([img_values, text_values], 1)

    def by_head(values, length):
        split = values.reshape(requests, length, heads_local, HD)
        return jnp.transpose(split, (0, 2, 1, 3)).reshape(requests * heads_local, length, HD)

    bundle = jnp.concatenate(
        [by_head(queries, patches), by_head(key_rows, block_len), by_head(value_rows, block_len)], 1
    )
    sources, bundle_rows = bundle.shape[0], bundle.shape[1]
    bundle = bundle.reshape(sources, bundle_rows // 2, 2 * HD)
    bundle = lax.all_to_all(bundle, ROW, 0, 0, tiled=True)
    bundle = bundle.reshape(sources, bundle_rows, HD)
    head_queries = bundle[:, :patches].reshape(sources * patches, HD)
    keys = bundle[:, patches : patches + block_len].reshape(sources * block_len, HD)
    values = bundle[:, patches + block_len :].reshape(sources * block_len, HD)

    request = lax.axis_index("rq")
    positions = jnp.arange(sources * block_len, dtype=jnp.int32)
    within = positions % block_len
    source_row = positions // block_len
    text_pos = source_row * text_rows + within - patches
    live_text = text_pos < lax.dynamic_index_in_dim(txt_len, request, keepdims=False)
    allowed = (within < patches) | live_text

    attended = attend_one(head_queries, keys, values, allowed).reshape(sources, patches, HD)
    attended = lax.all_to_all(attended, ROW, 0, 0, tiled=True)
    attended = jnp.transpose(
        attended.reshape(requests, heads_local, patches, HD), (0, 2, 1, 3)
    ).reshape(requests * patches, cols_local)

    partial_value = lax.dot_general(
        attended,
        weight_t,
        (((1,), (1,)), ((), ())),
        preferred_element_type=jnp.float32,
    )
    cols = lax.axis_size("col")
    col_index = lax.axis_index("col")
    shared_sum = halving_scatter(partial_value, cols, col_index)
    own_requests = requests // cols
    first = col_index * own_requests
    own_mods = lax.dynamic_slice_in_dim(img_mod, first, own_requests, 0)
    own_hidden = lax.dynamic_slice_in_dim(img_full, first, own_requests, 0).astype(jnp.float32)
    mixed = own_hidden + own_mods[:, 2:3, :] * shared_sum.reshape(own_requests, patches, D)
    modulated = (layer_norm(mixed) * (1.0 + own_mods[:, 4:5, :]) + own_mods[:, 3:4, :]).astype(
        jnp.bfloat16
    )
    velocity = jnp.einsum(
        "tcf,cof->to",
        modulated.reshape(own_requests * patches, slabs, D // slabs),
        final_slabs,
        preferred_element_type=jnp.float32,
    ).reshape(own_requests, patches, latent.shape[2])
    own_latent = lax.dynamic_slice_in_dim(latent, first, own_requests, 0)
    own_steps = lax.dynamic_slice_in_dim(step_idx, first, own_requests, 0)
    sigma_now = sigma_at(own_steps)[:, None, None]
    sigma_next = sigma_at(own_steps - 1)[:, None, None]
    advanced = own_latent + (sigma_next - sigma_now) * velocity
    denoised = own_latent - sigma_now * velocity
    both = doubling_gather(jnp.stack([advanced, denoised]), "col", COL_ORDER)
    both = jnp.moveaxis(both, 0, 1).reshape((2, requests) + both.shape[3:])
    advanced, denoised = both[0], both[1]
    return (advanced, denoised)


def solution(mesh):
    rows = mesh.shape["row"]
    cols = mesh.shape["col"]
    split = Mesh(mesh.devices.reshape(REQ, rows // REQ, cols), ("rq", "rm", "col"))
    in_specs = (
        P(None, ROW, "col"),
        P(None, ROW, "col"),
        P(None, ROW, None),
        P(),
        P(),
        P(None, None, "col"),
        P(None, None, "col"),
        P("col", ROW),
        P("col", None),
        P(),
        P(),
        P(),
    )
    out_specs = (P(None, ROW, None), P(None, ROW, None))
    return jax.shard_map(
        per_device, mesh=split, in_specs=in_specs, out_specs=out_specs, check_vma=False
    )
```

```python
import jax
import jax.numpy as jnp
from jax import lax
from jax.sharding import Mesh
from jax.sharding import PartitionSpec as P

D = 2432
HD = 64
STEPS = 28
REQ = 8

ROW = ("rq", "rm")

eps_norm = 1e-06
neg_fill = -1e30


def layer_norm(values):
    average = jnp.mean(values, -1, keepdims=True)
    centred = values - average
    variance = jnp.mean(centred * centred, -1, keepdims=True)
    return centred * lax.rsqrt(variance + eps_norm)


def rms_heads(values, scaling):
    reshaped = values.reshape(values.shape[:-1] + (values.shape[-1] // HD, HD))
    inverse = lax.rsqrt(jnp.mean(reshaped * reshaped, -1, keepdims=True) + eps_norm)
    return (reshaped * inverse * scaling).astype(jnp.bfloat16)


def sigma_at(indices):
    fraction = indices.astype(jnp.float32) / STEPS
    return 3.0 * fraction / (1.0 + 2.0 * fraction)


def doubling_gather(block, axis, order):
    size = lax.axis_size(axis)
    index = lax.axis_index(axis)
    bits = len(order)
    buffer = block[None]
    for bit in order:
        pairs = [(i, i ^ (1 << bit)) for i in range(size)]
        received = lax.ppermute(buffer, axis, pairs)
        upper = (index >> bit) % 2 == 1
        buffer = jnp.where(upper, jnp.stack([received, buffer]), jnp.stack([buffer, received]))
    done = list(reversed(order))
    buffer = buffer.reshape((2,) * bits + block.shape)
    perm = [done.index(bit) for bit in reversed(range(bits))]
    buffer = jnp.transpose(buffer, perm + list(range(bits, bits + block.ndim)))
    return buffer.reshape((size,) + block.shape)


COL_ORDER = [1, 0]


def gather_features(local):
    stacked = doubling_gather(local, "col", COL_ORDER)
    slabs = stacked.shape[0]
    moved = jnp.moveaxis(stacked, 0, -2)
    return moved.reshape(local.shape[:-1] + (slabs * local.shape[-1],))


def halving_scatter(partial, cols, col_index):
    rows = partial.shape[0] // cols
    chunks = partial.reshape((2, 2, rows) + partial.shape[1:])
    low = col_index % 2
    high = col_index // 2
    keep = lax.dynamic_index_in_dim(chunks, low, 1, keepdims=False)
    send = lax.dynamic_index_in_dim(chunks, 1 - low, 1, keepdims=False)
    pairs = [(i, i ^ 1) for i in range(cols)]
    halves = keep + lax.ppermute(send, "col", pairs)
    keep = lax.dynamic_index_in_dim(halves, high, 0, keepdims=False)
    send = lax.dynamic_index_in_dim(halves, 1 - high, 0, keepdims=False)
    pairs = [(i, i ^ 2) for i in range(cols)]
    received = lax.ppermute(send.astype(jnp.bfloat16), "col", pairs)
    return keep + received.astype(jnp.float32)


def attend_one(queries, keys, values, allowed):
    scores = jnp.dot(queries, keys.T, preferred_element_type=jnp.float32) * HD ** (-0.5)
    scores = jnp.where(allowed[None, :], scores, neg_fill)
    top_score = jnp.max(scores, -1, keepdims=True)
    exp_scores = jnp.where(allowed[None, :], jnp.exp(scores - top_score), 0.0)
    row_total = jnp.sum(exp_scores, -1, keepdims=True)
    weighted = jnp.dot(exp_scores.astype(jnp.bfloat16), values, preferred_element_type=jnp.float32)
    return (weighted / row_total).astype(jnp.bfloat16)


def per_device(
    img_hidden,
    txt_hidden,
    latent,
    img_mod,
    txt_mod,
    qkv_weight,
    txt_kv_weight,
    out_weight,
    final_weight,
    qk_gains,
    txt_len,
    step_idx,
):
    requests = img_hidden.shape[0]
    patches = img_hidden.shape[1]
    text_rows = txt_hidden.shape[1]
    cols_local = qkv_weight.shape[2]
    heads_local = cols_local // HD
    block_len = patches + text_rows

    weight_t = lax.all_gather(jnp.transpose(out_weight), ROW, axis=0, tiled=True)

    img_full = lax.optimization_barrier(gather_features(img_hidden))
    txt_rows = txt_hidden.reshape(requests * text_rows, -1)
    packed = jnp.concatenate([txt_rows, jnp.transpose(final_weight)], 0)
    packed = doubling_gather(packed, "col", COL_ORDER)
    slabs = packed.shape[0]
    txt_count = requests * text_rows
    txt_full = (
        jnp.moveaxis(packed[:, :txt_count], 0, -2)
        .reshape(txt_count, D)
        .reshape(requests, text_rows, D)
    )
    final_slabs = packed[:, txt_count:]
    normed = (layer_norm(img_full.astype(jnp.float32)) * (1.0 + img_mod[:, 1:2, :]) + img_mod[:, 0:1, :]).astype(
        jnp.bfloat16
    )
    flat_rows = normed.reshape(requests * patches, D)
    projected = jnp.einsum("td,cde->cte", flat_rows, qkv_weight, preferred_element_type=jnp.float32)
    queries = rms_heads(projected[0], qk_gains[0]).reshape(requests, patches, cols_local)
    img_keys = rms_heads(projected[1], qk_gains[1]).reshape(requests, patches, cols_local)
    img_values = projected[2].astype(jnp.bfloat16).reshape(requests, patches, cols_local)
    text_normed = (
        layer_norm(txt_full.astype(jnp.float32)) * (1.0 + txt_mod[:, 1:2, :]) + txt_mod[:, 0:1, :]
    ).astype(jnp.bfloat16)
    text_proj = jnp.einsum(
        "rtd,cde->crte", text_normed, txt_kv_weight, preferred_element_type=jnp.float32
    )
    text_keys = rms_heads(text_proj[0], qk_gains[2]).reshape(requests, text_rows, cols_local)
    text_values = text_proj[1].astype(jnp.bfloat16)
    key_rows = jnp.concatenate([img_keys, text_keys], 1)
    value_rows = jnp.concatenate([img_values, text_values], 1)

    def by_head(values, length):
        split = values.reshape(requests, length, heads_local, HD)
        moved = jnp.transpose(split, (0, 2, 1, 3))
        return moved.reshape(requests * heads_local, length // 2, 2 * HD)

    bundle = jnp.concatenate(
        [by_head(queries, patches), by_head(key_rows, block_len), by_head(value_rows, block_len)], 1
    )
    sources, bundle_rows = bundle.shape[0], 2 * bundle.shape[1]
    bundle = lax.all_to_all(bundle, ROW, 0, 0, tiled=True)
    bundle = bundle.reshape(sources, bundle_rows, HD)
    head_queries = bundle[:, :patches].reshape(sources * patches, HD)
    keys = bundle[:, patches : patches + block_len].reshape(sources * block_len, HD)
    values = bundle[:, patches + block_len :].reshape(sources * block_len, HD)

    request = lax.axis_index("rq")
    positions = jnp.arange(sources * block_len, dtype=jnp.int32)
    within = positions % block_len
    source_row = positions // block_len
    text_pos = source_row * text_rows + within - patches
    live_text = text_pos < lax.dynamic_index_in_dim(txt_len, request, keepdims=False)
    allowed = (within < patches) | live_text

    attended = attend_one(head_queries, keys, values, allowed).reshape(sources, patches, HD)
    attended = lax.all_to_all(attended, ROW, 0, 0, tiled=True)
    attended = jnp.transpose(
        attended.reshape(requests, heads_local, patches, HD), (0, 2, 1, 3)
    ).reshape(requests * patches, cols_local)

    partial_value = lax.dot_general(
        attended,
        weight_t,
        (((1,), (1,)), ((), ())),
        preferred_element_type=jnp.float32,
    )
    cols = lax.axis_size("col")
    col_index = lax.axis_index("col")
    shared_sum = halving_scatter(partial_value, cols, col_index)
    own_requests = requests // cols
    first = col_index * own_requests
    own_mods = lax.dynamic_slice_in_dim(img_mod, first, own_requests, 0)
    own_hidden = lax.dynamic_slice_in_dim(img_full, first, own_requests, 0).astype(jnp.float32)
    mixed = own_hidden + own_mods[:, 2:3, :] * shared_sum.reshape(own_requests, patches, D)
    modulated = (layer_norm(mixed) * (1.0 + own_mods[:, 4:5, :]) + own_mods[:, 3:4, :]).astype(
        jnp.bfloat16
    )
    velocity = jnp.einsum(
        "tcf,cof->to",
        modulated.reshape(own_requests * patches, slabs, D // slabs),
        final_slabs,
        preferred_element_type=jnp.float32,
    ).reshape(own_requests, patches, latent.shape[2])
    own_latent = lax.dynamic_slice_in_dim(latent, first, own_requests, 0)
    own_steps = lax.dynamic_slice_in_dim(step_idx, first, own_requests, 0)
    sigma_now = sigma_at(own_steps)[:, None, None]
    sigma_next = sigma_at(own_steps - 1)[:, None, None]
    advanced = own_latent + (sigma_next - sigma_now) * velocity
    denoised = own_latent - sigma_now * velocity
    both = doubling_gather(jnp.stack([advanced, denoised]), "col", COL_ORDER)
    both = jnp.moveaxis(both, 0, 1).reshape((2, requests) + both.shape[3:])
    advanced, denoised = both[0], both[1]
    return (advanced, denoised)


def solution(mesh):
    rows = mesh.shape["row"]
    cols = mesh.shape["col"]
    split = Mesh(mesh.devices.reshape(REQ, rows // REQ, cols), ("rq", "rm", "col"))
    in_specs = (
        P(None, ROW, "col"),
        P(None, ROW, "col"),
        P(None, ROW, None),
        P(),
        P(),
        P(None, None, "col"),
        P(None, None, "col"),
        P("col", ROW),
        P("col", None),
        P(),
        P(),
        P(),
    )
    out_specs = (P(None, ROW, None), P(None, ROW, None))
    return jax.shard_map(
        per_device, mesh=split, in_specs=in_specs, out_specs=out_specs, check_vma=False
    )
```

```python
import jax
import jax.numpy as jnp
from jax import lax
from jax.sharding import Mesh
from jax.sharding import PartitionSpec as P

D = 2432
HD = 64
STEPS = 28
REQ = 8

ROW = ("rq", "rm")

eps_norm = 1e-06
neg_fill = -1e30


def layer_norm(values):
    average = jnp.mean(values, -1, keepdims=True)
    centred = values - average
    variance = jnp.mean(centred * centred, -1, keepdims=True)
    return centred * lax.rsqrt(variance + eps_norm)


def rms_heads(values, scaling):
    reshaped = values.reshape(values.shape[:-1] + (values.shape[-1] // HD, HD))
    inverse = lax.rsqrt(jnp.mean(reshaped * reshaped, -1, keepdims=True) + eps_norm)
    return (reshaped * inverse * scaling).astype(jnp.bfloat16)


def sigma_at(indices):
    fraction = indices.astype(jnp.float32) / STEPS
    return 3.0 * fraction / (1.0 + 2.0 * fraction)


def doubling_gather(block, axis, order):
    size = lax.axis_size(axis)
    index = lax.axis_index(axis)
    bits = len(order)
    buffer = block[None]
    for bit in order:
        pairs = [(i, i ^ (1 << bit)) for i in range(size)]
        received = lax.ppermute(buffer, axis, pairs)
        upper = (index >> bit) % 2 == 1
        buffer = jnp.where(upper, jnp.stack([received, buffer]), jnp.stack([buffer, received]))
    done = list(reversed(order))
    buffer = buffer.reshape((2,) * bits + block.shape)
    perm = [done.index(bit) for bit in reversed(range(bits))]
    buffer = jnp.transpose(buffer, perm + list(range(bits, bits + block.ndim)))
    return buffer.reshape((size,) + block.shape)


COL_ORDER = [1, 0]


def gather_features(local):
    stacked = doubling_gather(local, "col", COL_ORDER)
    slabs = stacked.shape[0]
    moved = jnp.moveaxis(stacked, 0, -2)
    return moved.reshape(local.shape[:-1] + (slabs * local.shape[-1],))


def halving_scatter(partial, cols, col_index):
    rows = partial.shape[0] // cols
    chunks = partial.reshape((2, 2, rows) + partial.shape[1:])
    low = col_index % 2
    high = col_index // 2
    keep = lax.dynamic_index_in_dim(chunks, low, 1, keepdims=False)
    send = lax.dynamic_index_in_dim(chunks, 1 - low, 1, keepdims=False)
    pairs = [(i, i ^ 1) for i in range(cols)]
    halves = keep + lax.ppermute(send, "col", pairs)
    keep = lax.dynamic_index_in_dim(halves, high, 0, keepdims=False)
    send = lax.dynamic_index_in_dim(halves, 1 - high, 0, keepdims=False)
    pairs = [(i, i ^ 2) for i in range(cols)]
    received = lax.ppermute(send.astype(jnp.bfloat16), "col", pairs)
    return keep + received.astype(jnp.float32)


def attend_one(queries, keys, values, allowed):
    scores = jnp.dot(queries, keys.T, preferred_element_type=jnp.float32) * HD ** (-0.5)
    scores = jnp.where(allowed[None, :], scores, neg_fill)
    top_score = jnp.max(scores, -1, keepdims=True)
    exp_scores = jnp.where(allowed[None, :], jnp.exp(scores - top_score), 0.0)
    row_total = jnp.sum(exp_scores, -1, keepdims=True)
    weighted = jnp.dot(exp_scores.astype(jnp.bfloat16), values, preferred_element_type=jnp.float32)
    return (weighted / row_total).astype(jnp.bfloat16)


def per_device(
    img_hidden,
    txt_hidden,
    latent,
    img_mod,
    txt_mod,
    qkv_weight,
    txt_kv_weight,
    out_weight,
    final_weight,
    qk_gains,
    txt_len,
    step_idx,
):
    requests = img_hidden.shape[0]
    patches = img_hidden.shape[1]
    text_rows = txt_hidden.shape[1]
    cols_local = qkv_weight.shape[2]
    heads_local = cols_local // HD
    block_len = patches + text_rows

    weight_t = lax.all_gather(jnp.transpose(out_weight), ROW, axis=0, tiled=True)

    img_full = lax.optimization_barrier(gather_features(img_hidden))
    txt_rows = txt_hidden.reshape(requests * text_rows, -1)
    packed = jnp.concatenate([txt_rows, jnp.transpose(final_weight)], 0)
    packed = doubling_gather(packed, "col", COL_ORDER)
    slabs = packed.shape[0]
    txt_count = requests * text_rows
    txt_full = lax.optimization_barrier(
        jnp.moveaxis(packed[:, :txt_count], 0, -2).reshape(requests, text_rows, D)
    )
    final_slabs = packed[:, txt_count:]
    normed = (layer_norm(img_full.astype(jnp.float32)) * (1.0 + img_mod[:, 1:2, :]) + img_mod[:, 0:1, :]).astype(
        jnp.bfloat16
    )
    flat_rows = normed.reshape(requests * patches, D)
    projected = jnp.einsum("td,cde->cte", flat_rows, qkv_weight, preferred_element_type=jnp.float32)
    queries = rms_heads(projected[0], qk_gains[0]).reshape(requests, patches, cols_local)
    img_keys = rms_heads(projected[1], qk_gains[1]).reshape(requests, patches, cols_local)
    img_values = projected[2].astype(jnp.bfloat16).reshape(requests, patches, cols_local)
    text_normed = (
        layer_norm(txt_full.astype(jnp.float32)) * (1.0 + txt_mod[:, 1:2, :]) + txt_mod[:, 0:1, :]
    ).astype(jnp.bfloat16)
    text_proj = jnp.einsum(
        "rtd,cde->crte", text_normed, txt_kv_weight, preferred_element_type=jnp.float32
    )
    text_keys = rms_heads(text_proj[0], qk_gains[2]).reshape(requests, text_rows, cols_local)
    text_values = text_proj[1].astype(jnp.bfloat16)
    key_rows = jnp.concatenate([img_keys, text_keys], 1)
    value_rows = jnp.concatenate([img_values, text_values], 1)

    def by_head(values, length):
        split = values.reshape(requests, length, heads_local, HD)
        moved = jnp.transpose(split, (0, 2, 1, 3))
        return moved.reshape(requests * heads_local, length // 2, 2 * HD)

    bundle = jnp.concatenate(
        [by_head(queries, patches), by_head(key_rows, block_len), by_head(value_rows, block_len)], 1
    )
    sources, bundle_rows = bundle.shape[0], 2 * bundle.shape[1]
    bundle = lax.all_to_all(bundle, ROW, 0, 0, tiled=True)
    bundle = bundle.reshape(sources, bundle_rows, HD)
    head_queries = bundle[:, :patches].reshape(sources * patches, HD)
    keys = bundle[:, patches : patches + block_len].reshape(sources * block_len, HD)
    values = bundle[:, patches + block_len :].reshape(sources * block_len, HD)

    request = lax.axis_index("rq")
    positions = jnp.arange(sources * block_len, dtype=jnp.int32)
    within = positions % block_len
    source_row = positions // block_len
    text_pos = source_row * text_rows + within - patches
    live_text = text_pos < lax.dynamic_index_in_dim(txt_len, request, keepdims=False)
    allowed = (within < patches) | live_text

    attended = attend_one(head_queries, keys, values, allowed).reshape(sources, patches, HD)
    attended = lax.all_to_all(attended, ROW, 0, 0, tiled=True)
    attended = jnp.transpose(
        attended.reshape(requests, heads_local, patches, HD), (0, 2, 1, 3)
    ).reshape(requests * patches, cols_local)

    partial_value = lax.dot_general(
        attended,
        weight_t,
        (((1,), (1,)), ((), ())),
        preferred_element_type=jnp.float32,
    )
    cols = lax.axis_size("col")
    col_index = lax.axis_index("col")
    shared_sum = halving_scatter(partial_value, cols, col_index)
    own_requests = requests // cols
    first = col_index * own_requests
    own_mods = lax.dynamic_slice_in_dim(img_mod, first, own_requests, 0)
    own_hidden = lax.dynamic_slice_in_dim(img_full, first, own_requests, 0).astype(jnp.float32)
    mixed = own_hidden + own_mods[:, 2:3, :] * shared_sum.reshape(own_requests, patches, D)
    modulated = (layer_norm(mixed) * (1.0 + own_mods[:, 4:5, :]) + own_mods[:, 3:4, :]).astype(
        jnp.bfloat16
    )
    velocity = jnp.einsum(
        "tcf,cof->to",
        modulated.reshape(own_requests * patches, slabs, D // slabs),
        final_slabs,
        preferred_element_type=jnp.float32,
    ).reshape(own_requests, patches, latent.shape[2])
    own_latent = lax.dynamic_slice_in_dim(latent, first, own_requests, 0)
    own_steps = lax.dynamic_slice_in_dim(step_idx, first, own_requests, 0)
    sigma_now = sigma_at(own_steps)[:, None, None]
    sigma_next = sigma_at(own_steps - 1)[:, None, None]
    advanced = own_latent + (sigma_next - sigma_now) * velocity
    denoised = own_latent - sigma_now * velocity
    both = doubling_gather(jnp.stack([advanced, denoised]), "col", COL_ORDER)
    both = jnp.moveaxis(both, 0, 1).reshape((2, requests) + both.shape[3:])
    advanced, denoised = both[0], both[1]
    return (advanced, denoised)


def solution(mesh):
    rows = mesh.shape["row"]
    cols = mesh.shape["col"]
    split = Mesh(mesh.devices.reshape(REQ, rows // REQ, cols), ("rq", "rm", "col"))
    in_specs = (
        P(None, ROW, "col"),
        P(None, ROW, "col"),
        P(None, ROW, None),
        P(),
        P(),
        P(None, None, "col"),
        P(None, None, "col"),
        P("col", ROW),
        P("col", None),
        P(),
        P(),
        P(),
    )
    out_specs = (P(None, ROW, None), P(None, ROW, None))
    return jax.shard_map(
        per_device, mesh=split, in_specs=in_specs, out_specs=out_specs, check_vma=False
    )
```
